128 devices in a mesh: seq: 16 (over z, y), tp: 8 (over x, core).
Axes of the slice: x: 4, y: 4, z: 4, core: 2. Of those that a mesh axis runs over, the one named last changes fastest.
Arguments:
- tokens: bfloat16 [8192, 4096], P(('seq', 'tp')), may hold values from -24 to 24
- w_query: bfloat16 [4096, 4096], P(None, 'tp'), may hold values from -0.09375 to 0.09375
- w_key: bfloat16 [4096, 4096], P(None, 'tp'), may hold values from -0.09375 to 0.09375
- w_value: bfloat16 [4096, 4096], P(None, 'tp'), may hold values from -0.09375 to 0.09375
- w_out: bfloat16 [4096, 4096], P('tp'), may hold values from -0.09375 to 0.09375
- state_in: float32 [32, 128, 128], P('tp'), may hold values from -400 to 400
- grad_out: bfloat16 [8192, 4096], P(('seq', 'tp')), may hold values from -6 to 6
Outputs:
- mixed_out: bfloat16 [8192, 4096], P(('seq', 'tp'))
- input_grad: bfloat16 [8192, 4096], P(('seq', 'tp'))
- query_wgrad: float32 [4096, 4096], P('seq', 'tp')
- key_wgrad: float32 [4096, 4096], P('seq', 'tp')
- value_wgrad: float32 [4096, 4096], P('seq', 'tp')
- out_wgrad: float32 [4096, 4096], P('tp', 'seq')
- state_grad: float32 [32, 128, 128], P('tp', 'seq')
The draws below stay inside these ranges and needn't reach their ends.
All inputs are finite; a program needn't handle non-finite values.
Results may differ from the reference program's by a relative error of at most 0.02.
Values may be sent and summed in bfloat16 or wider, within the bound.
No kernel may reach another device: no remote copies, remote signals or barrier semaphores. Data moves between devices by JAX's collectives and lax.ppermute only.
A program may use at most 128 MiB of HBM per device.

```python
import jax
import jax.numpy as jnp
from jax import lax

D = 4096
H = 32
DK = 128
TOK_DEV = 512
TOKENS = 8192
N_TP = 8


def spiked(drawn, rng, source, target, shards_of, factor):
    owner, partner = [(jnp.arange(drawn.shape[position]) // (drawn.shape[position] // shards_of)).reshape([-1 if axis == position else 1 for axis in range(drawn.ndim)]) for position in (source, target)]
    chosen = jax.random.permutation(rng, shards_of)[partner]
    strong = (owner == chosen) | (owner == (partner + shards_of // 2) % shards_of)
    return jnp.where(strong, factor * drawn, drawn)


def levels(stream_key, dims, shards, low, largest):
    loudness = 1.0
    for dim, shards_of in shards:
        draws = jax.random.uniform(jax.random.fold_in(jax.random.fold_in(stream_key, 6), dim), (shards_of,), jnp.float32, low / len(shards), largest / len(shards))
        loudness = loudness * jnp.repeat(jnp.exp(draws), dims[dim] // shards_of).reshape((-1,) + (1,) * (len(dims) - 1 - dim))
    return loudness


def centred(own_key, dims, spread, reach, shards=(), kind=jnp.bfloat16):
    result = spread * jax.random.normal(own_key, dims, jnp.float32)
    if shards:
        result = result * levels(own_key, dims, shards, -0.22, 0.18)
    return jnp.clip(result, -reach, reach).astype(kind)


def noise_with(key, dims, deviation, bound, pieces, heavy, kind=jnp.bfloat16):
    entries = deviation * jax.random.normal(key, dims, jnp.float32)
    if pieces:
        entries = entries * levels(key, dims, pieces, -0.22, 0.18)
    return jnp.clip(spiked(entries, jax.random.fold_in(key, 3), *heavy), -bound, bound).astype(kind)


def setup_inputs(seed: int = 0) -> dict:
    key_list = jax.random.split(jax.random.key(seed), 8)
    tokens = noise_with(key_list[0], (TOKENS, D), 1.0, 24.0, ((0, 128),), (0, 1, 128, 5.5))
    w_query = centred(key_list[1], (D, D), D ** -0.5, 0.09375, ((1, 8),))
    w_key = centred(key_list[2], (D, D), D ** -0.5, 0.09375, ((1, 8),))
    w_value = centred(key_list[3], (D, D), D ** -0.5, 0.09375, ((1, 8),))
    w_out = centred(key_list[4], (D, D), D ** -0.5, 0.09375, ((0, 8),))
    state_in = centred(key_list[5], (H, DK, DK), 64.0, 400.0, ((0, 8),), jnp.float32)
    grad_out = centred(key_list[6], (TOKENS, D), 1.0, 6.0, ((0, 128),))
    return {"tokens": tokens, "w_query": w_query, "w_key": w_key, "w_value": w_value, "w_out": w_out, "state_in": state_in, "grad_out": grad_out}


HIGH = lax.Precision.HIGHEST

def causal_mask(length):
    row_ids = lax.broadcasted_iota(jnp.int32, (length, length), 0)
    col_ids = lax.broadcasted_iota(jnp.int32, (length, length), 1)
    return row_ids >= col_ids

def rounded(matrix):
    return lax.optimization_barrier(matrix.astype(jnp.bfloat16)).astype(jnp.float32)

def reference(tokens, w_query, w_key, w_value, w_out, state_in, grad_out):
    total = tokens.shape[0]
    head_count = state_in.shape[0]
    model_width = tokens.shape[1]
    query = jnp.dot(tokens, w_query, preferred_element_type=jnp.float32).astype(jnp.bfloat16)
    key_all = jnp.dot(tokens, w_key, preferred_element_type=jnp.float32).astype(jnp.bfloat16)
    value_all = jnp.dot(tokens, w_value, preferred_element_type=jnp.float32).astype(jnp.bfloat16)
    blocks = total // TOK_DEV

    def to_blocks(matrix):
        return matrix.astype(jnp.float32).reshape(blocks, TOK_DEV, head_count, -1)
    query_blk = to_blocks(query)
    key_blk = to_blocks(key_all)
    value_blk = to_blocks(value_all)
    mask = causal_mask(TOK_DEV)[None]

    def forward_block(state, inputs):
        query_b, key_b, value_b = inputs
        scores = jnp.einsum('thd,shd->hts', query_b, key_b, precision=HIGH)
        masked = jnp.where(mask, scores, 0.0)
        attn = jnp.einsum('hts,shd->thd', masked, value_b, precision=HIGH) + jnp.einsum('thd,hde->the', query_b, state, precision=HIGH)
        new_state = state + jnp.einsum('thd,the->hde', key_b, value_b, precision=HIGH)
        return (new_state, (attn, state))
    unused_state, (attn, before) = lax.scan(forward_block, state_in, (query_blk, key_blk, value_blk))
    inverse = lax.rsqrt(lax.optimization_barrier(jnp.mean(attn * attn, axis=-1, keepdims=True)) + 1e-05)
    normed = attn * inverse
    heads_out = normed.reshape(total, model_width).astype(jnp.bfloat16)
    group = model_width // N_TP
    mixed = jnp.zeros((total, model_width), jnp.float32)
    for group_id in range(N_TP):
        lower = group_id * group
        term = jnp.dot(heads_out[:, lower:lower + group], w_out[lower:lower + group, :], preferred_element_type=jnp.float32)
        mixed = mixed + rounded(term)
    mixed_out = mixed.astype(jnp.bfloat16)
    d_normed = jnp.dot(grad_out, w_out.T, preferred_element_type=jnp.float32).reshape(blocks, TOK_DEV, head_count, -1)
    d_attn = inverse * (d_normed - normed * lax.optimization_barrier(jnp.mean(d_normed * normed, axis=-1, keepdims=True)))

    def backward_block(later, inputs):
        query_b, key_b, value_b, adjoint_b, before_b = inputs
        scores = jnp.einsum('thd,shd->hts', query_b, key_b, precision=HIGH)
        masked = jnp.where(mask, scores, 0.0)
        mixed_s = jnp.where(mask, jnp.einsum('the,she->hts', adjoint_b, value_b, precision=HIGH), 0.0)
        grad_q = jnp.einsum('the,hde->thd', adjoint_b, before_b, precision=HIGH) + jnp.einsum('hts,shd->thd', mixed_s, key_b, precision=HIGH)
        grad_k = jnp.einsum('hts,thd->shd', mixed_s, query_b, precision=HIGH) + jnp.einsum('hde,she->shd', later, value_b, precision=HIGH)
        grad_v = jnp.einsum('hts,the->she', masked, adjoint_b, precision=HIGH) + jnp.einsum('hde,shd->she', later, key_b, precision=HIGH)
        new_later = later + jnp.einsum('thd,the->hde', query_b, adjoint_b, precision=HIGH)
        return (new_later, (grad_q, grad_k, grad_v))
    state_grad, (grad_q, grad_k, grad_v) = lax.scan(backward_block, jnp.zeros_like(state_in), (query_blk, key_blk, value_blk, d_attn, before), reverse=True)
    query_grad = grad_q.reshape(total, model_width).astype(jnp.bfloat16)
    key_grad = grad_k.reshape(total, model_width).astype(jnp.bfloat16)
    value_grad = grad_v.reshape(total, model_width).astype(jnp.bfloat16)
    inputs_sum = jnp.zeros((total, model_width), jnp.float32)
    for group_id in range(N_TP):
        lower = group_id * group
        term = jnp.dot(query_grad[:, lower:lower + group], w_query[:, lower:lower + group].T, preferred_element_type=jnp.float32)
        term = term + jnp.dot(key_grad[:, lower:lower + group], w_key[:, lower:lower + group].T, preferred_element_type=jnp.float32)
        term = term + jnp.dot(value_grad[:, lower:lower + group], w_value[:, lower:lower + group].T, preferred_element_type=jnp.float32)
        inputs_sum = inputs_sum + rounded(term)
    input_grad = inputs_sum.astype(jnp.bfloat16)
    query_acc = jnp.zeros((model_width, model_width), jnp.float32)
    key_acc = jnp.zeros((model_width, model_width), jnp.float32)
    value_acc = jnp.zeros((model_width, model_width), jnp.float32)
    out_acc = jnp.zeros((model_width, model_width), jnp.float32)
    for block_id in range(blocks):
        lower = block_id * TOK_DEV
        rows_b = tokens[lower:lower + TOK_DEV]
        query_acc = query_acc + rounded(jnp.dot(rows_b.T, query_grad[lower:lower + TOK_DEV], preferred_element_type=jnp.float32))
        key_acc = key_acc + rounded(jnp.dot(rows_b.T, key_grad[lower:lower + TOK_DEV], preferred_element_type=jnp.float32))
        value_acc = value_acc + rounded(jnp.dot(rows_b.T, value_grad[lower:lower + TOK_DEV], preferred_element_type=jnp.float32))
        out_acc = out_acc + rounded(jnp.dot(heads_out[lower:lower + TOK_DEV].T, grad_out[lower:lower + TOK_DEV], preferred_element_type=jnp.float32))
    grad_scale = lax.rsqrt(jnp.float32(total))
    return (mixed_out, input_grad, query_acc * grad_scale, key_acc * grad_scale, value_acc * grad_scale, out_acc * grad_scale, state_grad)
```

```python
import jax
import jax.numpy as jnp
from jax import lax
from jax.sharding import PartitionSpec as P

HIGH = lax.Precision.HIGHEST
ROWS_CONTRACT = (((0,), (0,)), ((), ()))
COLS_CONTRACT = (((1,), (1,)), ((), ()))


def scanned(array, axis):
    count = lax.axis_size(axis)
    place = lax.axis_index(axis)
    total = array
    before = jnp.zeros_like(array)
    after = jnp.zeros_like(array)
    step = 1
    while step < count:
        pairs = [(i, i ^ step) for i in range(count)]
        other = lax.ppermute(total, axis, pairs)
        upper = (place & step) != 0
        before = before + jnp.where(upper, other, 0.0)
        after = after + jnp.where(upper, 0.0, other)
        total = total + other
        step *= 2
    return before, after, total


def body(tokens, w_query, w_key, w_value, w_out, state_in, grad_out):
    head_count = state_in.shape[0]
    head_width = state_in.shape[1]
    rows_all = lax.all_gather(tokens, "tp", axis=0, tiled=True)
    shard_len = rows_all.shape[0]

    def head_split(matrix):
        return matrix.reshape(shard_len, head_count, head_width)

    query = jnp.dot(rows_all, w_query, preferred_element_type=jnp.float32).astype(jnp.bfloat16)
    key_all = jnp.dot(rows_all, w_key, preferred_element_type=jnp.float32).astype(jnp.bfloat16)
    value_all = jnp.dot(rows_all, w_value, preferred_element_type=jnp.float32).astype(jnp.bfloat16)
    query_heads = head_split(query)
    key_heads = head_split(key_all)
    value_heads = head_split(value_all)
    query_full = query_heads.astype(jnp.float32)
    key_full = key_heads.astype(jnp.float32)
    value_full = value_heads.astype(jnp.float32)
    local_kv = jnp.einsum(
        "thd,the->hde", key_heads, value_heads, preferred_element_type=jnp.float32
    )
    earlier, _, _ = scanned(local_kv, "seq")
    state_before = state_in + earlier
    row_ids = lax.broadcasted_iota(jnp.int32, (shard_len, shard_len), 0)
    col_ids = lax.broadcasted_iota(jnp.int32, (shard_len, shard_len), 1)
    mask = (row_ids >= col_ids)[None]
    scores = jnp.einsum("thd,shd->hts", query_heads, key_heads, preferred_element_type=jnp.float32)
    masked = jnp.where(mask, scores, 0.0)
    attn = jnp.einsum("hts,shd->thd", masked, value_full, precision=HIGH) + jnp.einsum(
        "thd,hde->the", query_full, state_before, precision=HIGH
    )
    inverse = lax.rsqrt(jnp.mean(attn * attn, axis=-1, keepdims=True) + 1e-05)
    normed = attn * inverse
    heads_out = normed.reshape(shard_len, head_count * head_width).astype(jnp.bfloat16)
    mixed_out = lax.psum_scatter(
        jnp.dot(heads_out, w_out, preferred_element_type=jnp.float32).astype(jnp.bfloat16),
        "tp",
        scatter_dimension=0,
        tiled=True,
    )
    grad_all = lax.all_gather(grad_out, "tp", axis=0, tiled=True)
    out_part = lax.dot_general(
        heads_out, grad_all, ROWS_CONTRACT, preferred_element_type=jnp.float32
    )
    d_normed = lax.dot_general(grad_all, w_out, COLS_CONTRACT, preferred_element_type=jnp.float32)
    d_normed = d_normed.reshape(shard_len, head_count, head_width)
    d_attn = inverse * (d_normed - normed * jnp.mean(d_normed * normed, axis=-1, keepdims=True))
    local_adj = jnp.einsum("thd,the->hde", query_full, d_attn, precision=HIGH)
    _, later, adj_total = scanned(local_adj, "seq")
    rows_per = head_width // lax.axis_size("seq")
    state_grad = lax.dynamic_slice_in_dim(
        adj_total, lax.axis_index("seq") * rows_per, rows_per, axis=1
    )
    mixed_s = jnp.where(mask, jnp.einsum("the,she->hts", d_attn, value_full, precision=HIGH), 0.0)
    grad_q = jnp.einsum("the,hde->thd", d_attn, state_before, precision=HIGH) + jnp.einsum(
        "hts,shd->thd", mixed_s, key_full, precision=HIGH
    )
    grad_k = jnp.einsum("hts,thd->shd", mixed_s, query_full, precision=HIGH) + jnp.einsum(
        "hde,she->shd", later, value_full, precision=HIGH
    )
    grad_v = jnp.einsum("hts,the->she", masked, d_attn, precision=HIGH) + jnp.einsum(
        "hde,shd->she", later, key_full, precision=HIGH
    )
    query_grad = grad_q.reshape(shard_len, head_count * head_width).astype(jnp.bfloat16)
    key_grad = grad_k.reshape(shard_len, head_count * head_width).astype(jnp.bfloat16)
    value_grad = grad_v.reshape(shard_len, head_count * head_width).astype(jnp.bfloat16)
    term = lax.dot_general(query_grad, w_query, COLS_CONTRACT, preferred_element_type=jnp.float32)
    term = term + lax.dot_general(
        key_grad, w_key, COLS_CONTRACT, preferred_element_type=jnp.float32
    )
    input_grad = lax.psum_scatter(
        (
            term
            + lax.dot_general(
                value_grad, w_value, COLS_CONTRACT, preferred_element_type=jnp.float32
            )
        ).astype(jnp.bfloat16),
        "tp",
        scatter_dimension=0,
        tiled=True,
    )
    query_part = lax.dot_general(
        rows_all, query_grad, ROWS_CONTRACT, preferred_element_type=jnp.float32
    )
    key_part = lax.dot_general(
        rows_all, key_grad, ROWS_CONTRACT, preferred_element_type=jnp.float32
    )
    value_part = lax.dot_general(
        rows_all, value_grad, ROWS_CONTRACT, preferred_element_type=jnp.float32
    )
    query_sum, key_sum, value_sum, out_summed = (
        lax.psum_scatter(
            query_part.astype(jnp.bfloat16), "seq", scatter_dimension=0, tiled=True
        ).astype(jnp.float32),
        lax.psum_scatter(
            key_part.astype(jnp.bfloat16), "seq", scatter_dimension=0, tiled=True
        ).astype(jnp.float32),
        lax.psum_scatter(
            value_part.astype(jnp.bfloat16), "seq", scatter_dimension=0, tiled=True
        ).astype(jnp.float32),
        lax.psum_scatter(
            out_part.astype(jnp.bfloat16), "seq", scatter_dimension=1, tiled=True
        ).astype(jnp.float32),
    )
    grad_scale = lax.rsqrt(jnp.float32(shard_len * lax.axis_size("seq")))
    return (
        mixed_out,
        input_grad,
        query_sum * grad_scale,
        key_sum * grad_scale,
        value_sum * grad_scale,
        out_summed * grad_scale,
        state_grad,
    )


def solution(mesh):
    return jax.shard_map(
        body,
        mesh=mesh,
        in_specs=(
            P(("seq", "tp"), None),
            P(None, "tp"),
            P(None, "tp"),
            P(None, "tp"),
            P("tp", None),
            P("tp", None, None),
            P(("seq", "tp"), None),
        ),
        out_specs=(
            P(("seq", "tp"), None),
            P(("seq", "tp"), None),
            P("seq", "tp"),
            P("seq", "tp"),
            P("seq", "tp"),
            P("tp", "seq"),
            P("tp", "seq", None),
        ),
        check_vma=False,
    )
```

```python
import jax
import jax.numpy as jnp
from jax import lax
from jax.sharding import PartitionSpec as P

HIGH = lax.Precision.HIGHEST
ROWS_CONTRACT = (((0,), (0,)), ((), ()))
COLS_CONTRACT = (((1,), (1,)), ((), ()))


def scanned(array, axis):
    count = lax.axis_size(axis)
    place = lax.axis_index(axis)
    total = array
    before = jnp.zeros_like(array)
    after = jnp.zeros_like(array)
    step = 1
    while step < count:
        pairs = [(i, i ^ step) for i in range(count)]
        other = lax.ppermute(total, axis, pairs)
        upper = (place & step) != 0
        before = before + jnp.where(upper, other, 0.0)
        after = after + jnp.where(upper, 0.0, other)
        total = total + other
        step *= 2
    return before, after, total


RING = 4


def ring_pairs(count, shift, inner):
    pairs = []
    for place in range(count):
        outer, within = divmod(place, RING)
        if inner:
            target = outer * RING + (within + shift) % RING
        else:
            target = ((outer + shift) % (count // RING)) * RING + within
        pairs.append((place, target))
    return pairs


def ring_reduce_scatter(pieces, axis, inner):
    count = lax.axis_size(axis)
    place = lax.axis_index(axis)
    ring = pieces.shape[0]
    pos = place % RING if inner else place // RING
    half = pieces.shape[-1] // 2
    ahead = pieces[..., :half]
    behind = pieces[..., half:]
    to_next = ring_pairs(count, 1, inner)
    to_prev = ring_pairs(count, -1, inner)

    def piece(source, index):
        return lax.dynamic_index_in_dim(source, index % ring, 0, False).astype(jnp.float32)

    acc_ahead = piece(ahead, pos - 1)
    acc_behind = piece(behind, pos + 1)
    for step in range(ring - 1):
        got_ahead = lax.ppermute(acc_ahead.astype(jnp.bfloat16), axis, to_next)
        got_behind = lax.ppermute(acc_behind.astype(jnp.bfloat16), axis, to_prev)
        acc_ahead = got_ahead.astype(jnp.float32) + piece(ahead, pos - 2 - step)
        acc_behind = got_behind.astype(jnp.float32) + piece(behind, pos + 2 + step)
    return jnp.concatenate([acc_ahead, acc_behind], axis=-1)


def grid_reduce_scatter(matrix, axis):
    count = lax.axis_size(axis)
    outer = count // RING
    rows = matrix.shape[0] // count
    cols = matrix.shape[1] // 2
    grid = matrix.reshape(outer, RING, rows, 2 * cols)
    first = grid[..., :cols]
    second = grid[..., cols:]
    first = ring_reduce_scatter(jnp.moveaxis(first, 1, 0), axis, True)
    second = ring_reduce_scatter(second, axis, False)
    first = ring_reduce_scatter(first.astype(jnp.bfloat16), axis, False)
    second = ring_reduce_scatter(second.astype(jnp.bfloat16), axis, True)
    return jnp.concatenate([first, second], axis=-1)


def body(tokens, w_query, w_key, w_value, w_out, state_in, grad_out):
    head_count = state_in.shape[0]
    head_width = state_in.shape[1]
    rows_all = lax.all_gather(tokens, "tp", axis=0, tiled=True)
    shard_len = rows_all.shape[0]

    def head_split(matrix):
        return matrix.reshape(shard_len, head_count, head_width)

    query = jnp.dot(rows_all, w_query, preferred_element_type=jnp.float32).astype(jnp.bfloat16)
    key_all = jnp.dot(rows_all, w_key, preferred_element_type=jnp.float32).astype(jnp.bfloat16)
    value_all = jnp.dot(rows_all, w_value, preferred_element_type=jnp.float32).astype(jnp.bfloat16)
    query_heads = head_split(query)
    key_heads = head_split(key_all)
    value_heads = head_split(value_all)
    query_full = query_heads.astype(jnp.float32)
    key_full = key_heads.astype(jnp.float32)
    value_full = value_heads.astype(jnp.float32)
    local_kv = jnp.einsum(
        "thd,the->hde", key_heads, value_heads, preferred_element_type=jnp.float32
    )
    earlier, _, _ = scanned(local_kv, "seq")
    state_before = state_in + earlier
    row_ids = lax.broadcasted_iota(jnp.int32, (shard_len, shard_len), 0)
    col_ids = lax.broadcasted_iota(jnp.int32, (shard_len, shard_len), 1)
    mask = (row_ids >= col_ids)[None]
    scores = jnp.einsum("thd,shd->hts", query_heads, key_heads, preferred_element_type=jnp.float32)
    masked = jnp.where(mask, scores, 0.0)
    attn = jnp.einsum("hts,shd->thd", masked, value_full, precision=HIGH) + jnp.einsum(
        "thd,hde->the", query_full, state_before, precision=HIGH
    )
    inverse = lax.rsqrt(jnp.mean(attn * attn, axis=-1, keepdims=True) + 1e-05)
    normed = attn * inverse
    heads_out = normed.reshape(shard_len, head_count * head_width).astype(jnp.bfloat16)
    mixed_out = lax.psum_scatter(
        jnp.dot(heads_out, w_out, preferred_element_type=jnp.float32).astype(jnp.bfloat16),
        "tp",
        scatter_dimension=0,
        tiled=True,
    )
    grad_all = lax.all_gather(grad_out, "tp", axis=0, tiled=True)
    out_part = lax.dot_general(
        heads_out, grad_all, ROWS_CONTRACT, preferred_element_type=jnp.float32
    )
    d_normed = lax.dot_general(grad_all, w_out, COLS_CONTRACT, preferred_element_type=jnp.float32)
    d_normed = d_normed.reshape(shard_len, head_count, head_width)
    d_attn = inverse * (d_normed - normed * jnp.mean(d_normed * normed, axis=-1, keepdims=True))
    local_adj = jnp.einsum("thd,the->hde", query_full, d_attn, precision=HIGH)
    _, later, adj_total = scanned(local_adj, "seq")
    rows_per = head_width // lax.axis_size("seq")
    state_grad = lax.dynamic_slice_in_dim(
        adj_total, lax.axis_index("seq") * rows_per, rows_per, axis=1
    )
    mixed_s = jnp.where(mask, jnp.einsum("the,she->hts", d_attn, value_full, precision=HIGH), 0.0)
    grad_q = jnp.einsum("the,hde->thd", d_attn, state_before, precision=HIGH) + jnp.einsum(
        "hts,shd->thd", mixed_s, key_full, precision=HIGH
    )
    grad_k = jnp.einsum("hts,thd->shd", mixed_s, query_full, precision=HIGH) + jnp.einsum(
        "hde,she->shd", later, value_full, precision=HIGH
    )
    grad_v = jnp.einsum("hts,the->she", masked, d_attn, precision=HIGH) + jnp.einsum(
        "hde,shd->she", later, key_full, precision=HIGH
    )
    query_grad = grad_q.reshape(shard_len, head_count * head_width).astype(jnp.bfloat16)
    key_grad = grad_k.reshape(shard_len, head_count * head_width).astype(jnp.bfloat16)
    value_grad = grad_v.reshape(shard_len, head_count * head_width).astype(jnp.bfloat16)
    term = lax.dot_general(query_grad, w_query, COLS_CONTRACT, preferred_element_type=jnp.float32)
    term = term + lax.dot_general(
        key_grad, w_key, COLS_CONTRACT, preferred_element_type=jnp.float32
    )
    input_grad = lax.psum_scatter(
        (
            term
            + lax.dot_general(
                value_grad, w_value, COLS_CONTRACT, preferred_element_type=jnp.float32
            )
        ).astype(jnp.bfloat16),
        "tp",
        scatter_dimension=0,
        tiled=True,
    )
    parts = jnp.concatenate(
        [
            lax.dot_general(rows_all, query_grad, ROWS_CONTRACT, preferred_element_type=jnp.float32),
            lax.dot_general(rows_all, key_grad, ROWS_CONTRACT, preferred_element_type=jnp.float32),
            lax.dot_general(rows_all, value_grad, ROWS_CONTRACT, preferred_element_type=jnp.float32),
            lax.dot_general(grad_all, heads_out, ROWS_CONTRACT, preferred_element_type=jnp.float32),
        ],
        axis=1,
    ).astype(jnp.bfloat16)
    summed = grid_reduce_scatter(parts, "seq")
    width = query_grad.shape[1]
    query_sum, key_sum, value_sum, out_sum = (
        summed[:, i * width : (i + 1) * width] for i in range(4)
    )
    out_summed = out_sum.T
    grad_scale = lax.rsqrt(jnp.float32(shard_len * lax.axis_size("seq")))
    return (
        mixed_out,
        input_grad,
        query_sum * grad_scale,
        key_sum * grad_scale,
        value_sum * grad_scale,
        out_summed * grad_scale,
        state_grad,
    )


def solution(mesh):
    return jax.shard_map(
        body,
        mesh=mesh,
        in_specs=(
            P(("seq", "tp"), None),
            P(None, "tp"),
            P(None, "tp"),
            P(None, "tp"),
            P("tp", None),
            P("tp", None, None),
            P(("seq", "tp"), None),
        ),
        out_specs=(
            P(("seq", "tp"), None),
            P(("seq", "tp"), None),
            P("seq", "tp"),
            P("seq", "tp"),
            P("seq", "tp"),
            P("tp", "seq"),
            P("tp", "seq", None),
        ),
        check_vma=False,
    )
```

```python
import jax
import jax.numpy as jnp
from jax import lax
from jax.sharding import PartitionSpec as P

HIGH = lax.Precision.HIGHEST
ROWS_CONTRACT = (((0,), (0,)), ((), ()))
COLS_CONTRACT = (((1,), (1,)), ((), ()))


def scanned(array, axis):
    count = lax.axis_size(axis)
    place = lax.axis_index(axis)
    total = array
    before = jnp.zeros_like(array)
    after = jnp.zeros_like(array)
    step = 1
    while step < count:
        pairs = [(i, i ^ step) for i in range(count)]
        other = lax.ppermute(total, axis, pairs)
        upper = (place & step) != 0
        before = before + jnp.where(upper, other, 0.0)
        after = after + jnp.where(upper, 0.0, other)
        total = total + other
        step *= 2
    return before, after, total


RING = 4


def ring_pairs(count, shift, inner):
    pairs = []
    for place in range(count):
        outer, within = divmod(place, RING)
        if inner:
            target = outer * RING + (within + shift) % RING
        else:
            target = ((outer + shift) % (count // RING)) * RING + within
        pairs.append((place, target))
    return pairs


def ring_reduce_scatter(ahead, behind, axis, inner, along):
    count = lax.axis_size(axis)
    place = lax.axis_index(axis)
    ring = ahead.shape[along]
    pos = place % RING if inner else place // RING
    to_next = ring_pairs(count, 1, inner)
    to_prev = ring_pairs(count, -1, inner)

    def piece(source, index):
        return lax.dynamic_index_in_dim(source, index % ring, along, False).astype(jnp.float32)

    acc_ahead = piece(ahead, pos - 1)
    acc_behind = piece(behind, pos + 1)
    for step in range(ring - 1):
        got_ahead = lax.ppermute(acc_ahead.astype(jnp.bfloat16), axis, to_next)
        got_behind = lax.ppermute(acc_behind.astype(jnp.bfloat16), axis, to_prev)
        acc_ahead = got_ahead.astype(jnp.float32) + piece(ahead, pos - 2 - step)
        acc_behind = got_behind.astype(jnp.float32) + piece(behind, pos + 2 + step)
    return acc_ahead, acc_behind


def grid_reduce_scatter(first, second, third, fourth, axis):
    count = lax.axis_size(axis)
    outer = count // RING

    def grid(matrix):
        return matrix.astype(jnp.bfloat16).reshape(outer, RING, matrix.shape[0] // count, matrix.shape[1])

    first, second = ring_reduce_scatter(grid(first), grid(second), axis, True, 1)
    third, fourth = ring_reduce_scatter(grid(third), grid(fourth), axis, False, 0)
    first, second = ring_reduce_scatter(
        first.astype(jnp.bfloat16), second.astype(jnp.bfloat16), axis, False, 0
    )
    third, fourth = ring_reduce_scatter(
        third.astype(jnp.bfloat16), fourth.astype(jnp.bfloat16), axis, True, 0
    )
    return first, second, third, fourth


def body(tokens, w_query, w_key, w_value, w_out, state_in, grad_out):
    head_count = state_in.shape[0]
    head_width = state_in.shape[1]
    rows_all = lax.all_gather(tokens, "tp", axis=0, tiled=True)
    shard_len = rows_all.shape[0]

    def head_split(matrix):
        return matrix.reshape(shard_len, head_count, head_width)

    query = jnp.dot(rows_all, w_query, preferred_element_type=jnp.float32).astype(jnp.bfloat16)
    key_all = jnp.dot(rows_all, w_key, preferred_element_type=jnp.float32).astype(jnp.bfloat16)
    value_all = jnp.dot(rows_all, w_value, preferred_element_type=jnp.float32).astype(jnp.bfloat16)
    query_heads = head_split(query)
    key_heads = head_split(key_all)
    value_heads = head_split(value_all)
    query_full = query_heads.astype(jnp.float32)
    key_full = key_heads.astype(jnp.float32)
    value_full = value_heads.astype(jnp.float32)
    local_kv = jnp.einsum(
        "thd,the->hde", key_heads, value_heads, preferred_element_type=jnp.float32
    )
    earlier, _, _ = scanned(local_kv, "seq")
    state_before = state_in + earlier
    row_ids = lax.broadcasted_iota(jnp.int32, (shard_len, shard_len), 0)
    col_ids = lax.broadcasted_iota(jnp.int32, (shard_len, shard_len), 1)
    mask = (row_ids >= col_ids)[None]
    scores = jnp.einsum("thd,shd->hts", query_heads, key_heads, preferred_element_type=jnp.float32)
    masked = jnp.where(mask, scores, 0.0)
    attn = jnp.einsum("hts,shd->thd", masked, value_full, precision=HIGH) + jnp.einsum(
        "thd,hde->the", query_full, state_before, precision=HIGH
    )
    inverse = lax.rsqrt(jnp.mean(attn * attn, axis=-1, keepdims=True) + 1e-05)
    normed = attn * inverse
    heads_out = normed.reshape(shard_len, head_count * head_width).astype(jnp.bfloat16)
    mixed_out = lax.psum_scatter(
        jnp.dot(heads_out, w_out, preferred_element_type=jnp.float32).astype(jnp.bfloat16),
        "tp",
        scatter_dimension=0,
        tiled=True,
    )
    grad_all = lax.all_gather(grad_out, "tp", axis=0, tiled=True)
    d_normed = lax.dot_general(grad_all, w_out, COLS_CONTRACT, preferred_element_type=jnp.float32)
    d_normed = d_normed.reshape(shard_len, head_count, head_width)
    d_attn = inverse * (d_normed - normed * jnp.mean(d_normed * normed, axis=-1, keepdims=True))
    local_adj = jnp.einsum("thd,the->hde", query_full, d_attn, precision=HIGH)
    _, later, adj_total = scanned(local_adj, "seq")
    rows_per = head_width // lax.axis_size("seq")
    state_grad = lax.dynamic_slice_in_dim(
        adj_total, lax.axis_index("seq") * rows_per, rows_per, axis=1
    )
    mixed_s = jnp.where(mask, jnp.einsum("the,she->hts", d_attn, value_full, precision=HIGH), 0.0)
    grad_q = jnp.einsum("the,hde->thd", d_attn, state_before, precision=HIGH) + jnp.einsum(
        "hts,shd->thd", mixed_s, key_full, precision=HIGH
    )
    grad_k = jnp.einsum("hts,thd->shd", mixed_s, query_full, precision=HIGH) + jnp.einsum(
        "hde,she->shd", later, value_full, precision=HIGH
    )
    grad_v = jnp.einsum("hts,the->she", masked, d_attn, precision=HIGH) + jnp.einsum(
        "hde,shd->she", later, key_full, precision=HIGH
    )
    query_grad = grad_q.reshape(shard_len, head_count * head_width).astype(jnp.bfloat16)
    key_grad = grad_k.reshape(shard_len, head_count * head_width).astype(jnp.bfloat16)
    value_grad = grad_v.reshape(shard_len, head_count * head_width).astype(jnp.bfloat16)
    term = lax.dot_general(query_grad, w_query, COLS_CONTRACT, preferred_element_type=jnp.float32)
    term = term + lax.dot_general(
        key_grad, w_key, COLS_CONTRACT, preferred_element_type=jnp.float32
    )
    input_grad = lax.psum_scatter(
        (
            term
            + lax.dot_general(
                value_grad, w_value, COLS_CONTRACT, preferred_element_type=jnp.float32
            )
        ).astype(jnp.bfloat16),
        "tp",
        scatter_dimension=0,
        tiled=True,
    )
    query_sum, key_sum, value_sum, out_sum = grid_reduce_scatter(
        lax.dot_general(rows_all, query_grad, ROWS_CONTRACT, preferred_element_type=jnp.float32),
        lax.dot_general(rows_all, key_grad, ROWS_CONTRACT, preferred_element_type=jnp.float32),
        lax.dot_general(rows_all, value_grad, ROWS_CONTRACT, preferred_element_type=jnp.float32),
        lax.dot_general(grad_all, heads_out, ROWS_CONTRACT, preferred_element_type=jnp.float32),
        "seq",
    )
    out_summed = out_sum.T
    grad_scale = lax.rsqrt(jnp.float32(shard_len * lax.axis_size("seq")))
    return (
        mixed_out,
        input_grad,
        query_sum * grad_scale,
        key_sum * grad_scale,
        value_sum * grad_scale,
        out_summed * grad_scale,
        state_grad,
    )


def solution(mesh):
    return jax.shard_map(
        body,
        mesh=mesh,
        in_specs=(
            P(("seq", "tp"), None),
            P(None, "tp"),
            P(None, "tp"),
            P(None, "tp"),
            P("tp", None),
            P("tp", None, None),
            P(("seq", "tp"), None),
        ),
        out_specs=(
            P(("seq", "tp"), None),
            P(("seq", "tp"), None),
            P("seq", "tp"),
            P("seq", "tp"),
            P("seq", "tp"),
            P("tp", "seq"),
            P("tp", "seq", None),
        ),
        check_vma=False,
    )
```

```python
import jax
import jax.numpy as jnp
from jax import lax
from jax.sharding import PartitionSpec as P

HIGH = lax.Precision.HIGHEST
ROWS_CONTRACT = (((0,), (0,)), ((), ()))
COLS_CONTRACT = (((1,), (1,)), ((), ()))


def scanned(array, axis):
    count = lax.axis_size(axis)
    place = lax.axis_index(axis)
    total = array
    before = jnp.zeros_like(array)
    after = jnp.zeros_like(array)
    step = 1
    while step < count:
        pairs = [(i, i ^ step) for i in range(count)]
        other = lax.ppermute(total, axis, pairs)
        upper = (place & step) != 0
        before = before + jnp.where(upper, other, 0.0)
        after = after + jnp.where(upper, 0.0, other)
        total = total + other
        step *= 2
    return before, after, total


RING = 4


def ring_pairs(count, shift, inner):
    pairs = []
    for place in range(count):
        outer, within = divmod(place, RING)
        if inner:
            target = outer * RING + (within + shift) % RING
        else:
            target = ((outer + shift) % (count // RING)) * RING + within
        pairs.append((place, target))
    return pairs


def ring_reduce_scatter(ahead, behind, axis, inner):
    count = lax.axis_size(axis)
    place = lax.axis_index(axis)
    size = ahead.shape[0] // RING
    pos = place % RING if inner else place // RING
    to_next = ring_pairs(count, 1, inner)
    to_prev = ring_pairs(count, -1, inner)

    def piece(source, index):
        return lax.dynamic_slice_in_dim(source, (index % RING) * size, size, 0).astype(jnp.float32)

    acc_ahead = piece(ahead, pos - 1)
    acc_behind = piece(behind, pos + 1)
    for step in range(RING - 1):
        got_ahead = lax.ppermute(acc_ahead.astype(jnp.bfloat16), axis, to_next)
        got_behind = lax.ppermute(acc_behind.astype(jnp.bfloat16), axis, to_prev)
        acc_ahead = got_ahead.astype(jnp.float32) + piece(ahead, pos - 2 - step)
        acc_behind = got_behind.astype(jnp.float32) + piece(behind, pos + 2 + step)
    return acc_ahead, acc_behind


def grid_reduce_scatter(first, second, third, fourth, axis):
    first, second = ring_reduce_scatter(first, second, axis, True)
    third, fourth = ring_reduce_scatter(third, fourth, axis, False)
    first, second = ring_reduce_scatter(
        first.astype(jnp.bfloat16), second.astype(jnp.bfloat16), axis, False
    )
    third, fourth = ring_reduce_scatter(
        third.astype(jnp.bfloat16), fourth.astype(jnp.bfloat16), axis, True
    )
    return first, second, third, fourth


def body(tokens, w_query, w_key, w_value, w_out, state_in, grad_out):
    head_count = state_in.shape[0]
    head_width = state_in.shape[1]
    rows_all = lax.all_gather(tokens, "tp", axis=0, tiled=True)
    shard_len = rows_all.shape[0]

    def head_split(matrix):
        return matrix.reshape(shard_len, head_count, head_width)

    query = jnp.dot(rows_all, w_query, preferred_element_type=jnp.float32).astype(jnp.bfloat16)
    key_all = jnp.dot(rows_all, w_key, preferred_element_type=jnp.float32).astype(jnp.bfloat16)
    value_all = jnp.dot(rows_all, w_value, preferred_element_type=jnp.float32).astype(jnp.bfloat16)
    query_heads = head_split(query)
    key_heads = head_split(key_all)
    value_heads = head_split(value_all)
    query_full = query_heads.astype(jnp.float32)
    key_full = key_heads.astype(jnp.float32)
    value_full = value_heads.astype(jnp.float32)
    local_kv = jnp.einsum(
        "thd,the->hde", key_heads, value_heads, preferred_element_type=jnp.float32
    )
    earlier, _, _ = scanned(local_kv, "seq")
    state_before = state_in + earlier
    row_ids = lax.broadcasted_iota(jnp.int32, (shard_len, shard_len), 0)
    col_ids = lax.broadcasted_iota(jnp.int32, (shard_len, shard_len), 1)
    mask = (row_ids >= col_ids)[None]
    scores = jnp.einsum("thd,shd->hts", query_heads, key_heads, preferred_element_type=jnp.float32)
    masked = jnp.where(mask, scores, 0.0)
    attn = jnp.einsum("hts,shd->thd", masked, value_full, precision=HIGH) + jnp.einsum(
        "thd,hde->the", query_full, state_before, precision=HIGH
    )
    inverse = lax.rsqrt(jnp.mean(attn * attn, axis=-1, keepdims=True) + 1e-05)
    normed = attn * inverse
    heads_out = normed.reshape(shard_len, head_count * head_width).astype(jnp.bfloat16)
    mixed_out = lax.psum_scatter(
        jnp.dot(heads_out, w_out, preferred_element_type=jnp.float32).astype(jnp.bfloat16),
        "tp",
        scatter_dimension=0,
        tiled=True,
    )
    grad_all = lax.all_gather(grad_out, "tp", axis=0, tiled=True)
    d_normed = lax.dot_general(grad_all, w_out, COLS_CONTRACT, preferred_element_type=jnp.float32)
    d_normed = d_normed.reshape(shard_len, head_count, head_width)
    d_attn = inverse * (d_normed - normed * jnp.mean(d_normed * normed, axis=-1, keepdims=True))
    local_adj = jnp.einsum("thd,the->hde", query_full, d_attn, precision=HIGH)
    _, later, adj_total = scanned(local_adj, "seq")
    rows_per = head_width // lax.axis_size("seq")
    state_grad = lax.dynamic_slice_in_dim(
        adj_total, lax.axis_index("seq") * rows_per, rows_per, axis=1
    )
    mixed_s = jnp.where(mask, jnp.einsum("the,she->hts", d_attn, value_full, precision=HIGH), 0.0)
    grad_q = jnp.einsum("the,hde->thd", d_attn, state_before, precision=HIGH) + jnp.einsum(
        "hts,shd->thd", mixed_s, key_full, precision=HIGH
    )
    grad_k = jnp.einsum("hts,thd->shd", mixed_s, query_full, precision=HIGH) + jnp.einsum(
        "hde,she->shd", later, value_full, precision=HIGH
    )
    grad_v = jnp.einsum("hts,the->she", masked, d_attn, precision=HIGH) + jnp.einsum(
        "hde,shd->she", later, key_full, precision=HIGH
    )
    query_grad = grad_q.reshape(shard_len, head_count * head_width).astype(jnp.bfloat16)
    key_grad = grad_k.reshape(shard_len, head_count * head_width).astype(jnp.bfloat16)
    value_grad = grad_v.reshape(shard_len, head_count * head_width).astype(jnp.bfloat16)
    term = lax.dot_general(query_grad, w_query, COLS_CONTRACT, preferred_element_type=jnp.float32)
    term = term + lax.dot_general(
        key_grad, w_key, COLS_CONTRACT, preferred_element_type=jnp.float32
    )
    input_grad = lax.psum_scatter(
        (
            term
            + lax.dot_general(
                value_grad, w_value, COLS_CONTRACT, preferred_element_type=jnp.float32
            )
        ).astype(jnp.bfloat16),
        "tp",
        scatter_dimension=0,
        tiled=True,
    )
    outer = lax.axis_size("seq") // RING
    rows_swapped = (
        rows_all.reshape(shard_len, outer, RING, -1)
        .transpose(0, 2, 1, 3)
        .reshape(shard_len, -1)
    )
    query_sum, key_sum, value_sum, out_sum = grid_reduce_scatter(
        lax.dot_general(rows_swapped, query_grad, ROWS_CONTRACT, preferred_element_type=jnp.bfloat16),
        lax.dot_general(rows_swapped, key_grad, ROWS_CONTRACT, preferred_element_type=jnp.bfloat16),
        lax.dot_general(rows_all, value_grad, ROWS_CONTRACT, preferred_element_type=jnp.bfloat16),
        lax.dot_general(grad_all, heads_out, ROWS_CONTRACT, preferred_element_type=jnp.bfloat16),
        "seq",
    )
    out_summed = out_sum.T
    grad_scale = lax.rsqrt(jnp.float32(shard_len * lax.axis_size("seq")))
    return (
        mixed_out,
        input_grad,
        query_sum.astype(jnp.float32) * grad_scale,
        key_sum.astype(jnp.float32) * grad_scale,
        value_sum.astype(jnp.float32) * grad_scale,
        out_summed.astype(jnp.float32) * grad_scale,
        state_grad,
    )


def solution(mesh):
    return jax.shard_map(
        body,
        mesh=mesh,
        in_specs=(
            P(("seq", "tp"), None),
            P(None, "tp"),
            P(None, "tp"),
            P(None, "tp"),
            P("tp", None),
            P("tp", None, None),
            P(("seq", "tp"), None),
        ),
        out_specs=(
            P(("seq", "tp"), None),
            P(("seq", "tp"), None),
            P("seq", "tp"),
            P("seq", "tp"),
            P("seq", "tp"),
            P("tp", "seq"),
            P("tp", "seq", None),
        ),
        check_vma=False,
    )
```

```python
import jax
import jax.numpy as jnp
from jax import lax
from jax.sharding import PartitionSpec as P

HIGH = lax.Precision.HIGHEST
ROWS_CONTRACT = (((0,), (0,)), ((), ()))
COLS_CONTRACT = (((1,), (1,)), ((), ()))


def scanned(array, axis):
    count = lax.axis_size(axis)
    place = lax.axis_index(axis)
    total = array
    before = jnp.zeros_like(array)
    after = jnp.zeros_like(array)
    step = 1
    while step < count:
        pairs = [(i, i ^ step) for i in range(count)]
        other = lax.ppermute(total, axis, pairs)
        upper = (place & step) != 0
        before = before + jnp.where(upper, other, 0.0)
        after = after + jnp.where(upper, 0.0, other)
        total = total + other
        step *= 2
    return before, after, total


RING = 4


def ring_pairs(count, shift, inner):
    pairs = []
    for place in range(count):
        outer, within = divmod(place, RING)
        if inner:
            target = outer * RING + (within + shift) % RING
        else:
            target = ((outer + shift) % (count // RING)) * RING + within
        pairs.append((place, target))
    return pairs


def ring_reduce_scatter(pieces, axis, inner, shift):
    count = lax.axis_size(axis)
    place = lax.axis_index(axis)
    size = pieces.shape[0] // RING
    pos = place % RING if inner else place // RING
    pairs = ring_pairs(count, shift, inner)

    def piece(index):
        return lax.dynamic_slice_in_dim(pieces, (index % RING) * size, size, 0).astype(jnp.float32)

    acc = piece(pos - shift)
    for step in range(RING - 1):
        got = lax.ppermute(acc.astype(jnp.bfloat16), axis, pairs)
        acc = got.astype(jnp.float32) + piece(pos - (2 + step) * shift)
    return acc


def grid_reduce_scatter(partial, axis, inner_first, shift):
    partial = ring_reduce_scatter(partial, axis, inner_first, shift)
    return ring_reduce_scatter(partial.astype(jnp.bfloat16), axis, not inner_first, shift)


def body(tokens, w_query, w_key, w_value, w_out, state_in, grad_out):
    head_count = state_in.shape[0]
    head_width = state_in.shape[1]
    rows_all = lax.all_gather(tokens, "tp", axis=0, tiled=True)
    shard_len = rows_all.shape[0]

    def head_split(matrix):
        return matrix.reshape(shard_len, head_count, head_width)

    query = jnp.dot(rows_all, w_query, preferred_element_type=jnp.float32).astype(jnp.bfloat16)
    key_all = jnp.dot(rows_all, w_key, preferred_element_type=jnp.float32).astype(jnp.bfloat16)
    value_all = jnp.dot(rows_all, w_value, preferred_element_type=jnp.float32).astype(jnp.bfloat16)
    query_heads = head_split(query)
    key_heads = head_split(key_all)
    value_heads = head_split(value_all)
    query_full = query_heads.astype(jnp.float32)
    key_full = key_heads.astype(jnp.float32)
    value_full = value_heads.astype(jnp.float32)
    local_kv = jnp.einsum(
        "thd,the->hde", key_heads, value_heads, preferred_element_type=jnp.float32
    )
    earlier, _, _ = scanned(local_kv, "seq")
    state_before = state_in + earlier
    row_ids = lax.broadcasted_iota(jnp.int32, (shard_len, shard_len), 0)
    col_ids = lax.broadcasted_iota(jnp.int32, (shard_len, shard_len), 1)
    mask = (row_ids >= col_ids)[None]
    scores = jnp.einsum("thd,shd->hts", query_heads, key_heads, preferred_element_type=jnp.float32)
    masked = jnp.where(mask, scores, 0.0)
    attn = jnp.einsum("hts,shd->thd", masked, value_full, precision=HIGH) + jnp.einsum(
        "thd,hde->the", query_full, state_before, precision=HIGH
    )
    inverse = lax.rsqrt(jnp.mean(attn * attn, axis=-1, keepdims=True) + 1e-05)
    normed = attn * inverse
    heads_out = normed.reshape(shard_len, head_count * head_width).astype(jnp.bfloat16)
    mixed_out = lax.psum_scatter(
        jnp.dot(heads_out, w_out, preferred_element_type=jnp.float32).astype(jnp.bfloat16),
        "tp",
        scatter_dimension=0,
        tiled=True,
    )
    grad_all = lax.all_gather(grad_out, "tp", axis=0, tiled=True)
    d_normed = lax.dot_general(grad_all, w_out, COLS_CONTRACT, preferred_element_type=jnp.float32)
    d_normed = d_normed.reshape(shard_len, head_count, head_width)
    d_attn = inverse * (d_normed - normed * jnp.mean(d_normed * normed, axis=-1, keepdims=True))
    local_adj = jnp.einsum("thd,the->hde", query_full, d_attn, precision=HIGH)
    _, later, adj_total = scanned(local_adj, "seq")
    rows_per = head_width // lax.axis_size("seq")
    state_grad = lax.dynamic_slice_in_dim(
        adj_total, lax.axis_index("seq") * rows_per, rows_per, axis=1
    )
    mixed_s = jnp.where(mask, jnp.einsum("the,she->hts", d_attn, value_full, precision=HIGH), 0.0)
    grad_q = jnp.einsum("the,hde->thd", d_attn, state_before, precision=HIGH) + jnp.einsum(
        "hts,shd->thd", mixed_s, key_full, precision=HIGH
    )
    grad_k = jnp.einsum("hts,thd->shd", mixed_s, query_full, precision=HIGH) + jnp.einsum(
        "hde,she->shd", later, value_full, precision=HIGH
    )
    grad_v = jnp.einsum("hts,the->she", masked, d_attn, precision=HIGH) + jnp.einsum(
        "hde,shd->she", later, key_full, precision=HIGH
    )
    query_grad = grad_q.reshape(shard_len, head_count * head_width).astype(jnp.bfloat16)
    key_grad = grad_k.reshape(shard_len, head_count * head_width).astype(jnp.bfloat16)
    value_grad = grad_v.reshape(shard_len, head_count * head_width).astype(jnp.bfloat16)
    term = lax.dot_general(query_grad, w_query, COLS_CONTRACT, preferred_element_type=jnp.float32)
    term = term + lax.dot_general(
        key_grad, w_key, COLS_CONTRACT, preferred_element_type=jnp.float32
    )
    input_grad = lax.psum_scatter(
        (
            term
            + lax.dot_general(
                value_grad, w_value, COLS_CONTRACT, preferred_element_type=jnp.float32
            )
        ).astype(jnp.bfloat16),
        "tp",
        scatter_dimension=0,
        tiled=True,
    )
    outer = lax.axis_size("seq") // RING
    rows_swapped = (
        rows_all.reshape(shard_len, outer, RING, -1)
        .transpose(0, 2, 1, 3)
        .reshape(shard_len, -1)
    )
    out_sum = grid_reduce_scatter(
        lax.dot_general(grad_all, heads_out, ROWS_CONTRACT, preferred_element_type=jnp.bfloat16),
        "seq",
        False,
        -1,
    )
    query_sum = grid_reduce_scatter(
        lax.dot_general(rows_swapped, query_grad, ROWS_CONTRACT, preferred_element_type=jnp.bfloat16),
        "seq",
        True,
        1,
    )
    key_sum = grid_reduce_scatter(
        lax.dot_general(rows_swapped, key_grad, ROWS_CONTRACT, preferred_element_type=jnp.bfloat16),
        "seq",
        True,
        -1,
    )
    value_sum = grid_reduce_scatter(
        lax.dot_general(rows_all, value_grad, ROWS_CONTRACT, preferred_element_type=jnp.bfloat16),
        "seq",
        False,
        1,
    )
    out_summed = out_sum.T
    grad_scale = lax.rsqrt(jnp.float32(shard_len * lax.axis_size("seq")))
    return (
        mixed_out,
        input_grad,
        query_sum.astype(jnp.float32) * grad_scale,
        key_sum.astype(jnp.float32) * grad_scale,
        value_sum.astype(jnp.float32) * grad_scale,
        out_summed.astype(jnp.float32) * grad_scale,
        state_grad,
    )


def solution(mesh):
    return jax.shard_map(
        body,
        mesh=mesh,
        in_specs=(
            P(("seq", "tp"), None),
            P(None, "tp"),
            P(None, "tp"),
            P(None, "tp"),
            P("tp", None),
            P("tp", None, None),
            P(("seq", "tp"), None),
        ),
        out_specs=(
            P(("seq", "tp"), None),
            P(("seq", "tp"), None),
            P("seq", "tp"),
            P("seq", "tp"),
            P("seq", "tp"),
            P("tp", "seq"),
            P("tp", "seq", None),
        ),
        check_vma=False,
    )
```

```python
import jax
import jax.numpy as jnp
from jax import lax
from jax.sharding import PartitionSpec as P

HIGH = lax.Precision.HIGHEST
ROWS_CONTRACT = (((0,), (0,)), ((), ()))
COLS_CONTRACT = (((1,), (1,)), ((), ()))


RING = 4


def ring_pairs(count, shift, inner):
    pairs = []
    for place in range(count):
        outer, within = divmod(place, RING)
        if inner:
            target = outer * RING + (within + shift) % RING
        else:
            target = ((outer + shift) % (count // RING)) * RING + within
        pairs.append((place, target))
    return pairs


def scanned(array, axis):
    count = lax.axis_size(axis)
    place = lax.axis_index(axis)
    before = jnp.zeros_like(array)
    after = jnp.zeros_like(array)
    total = array
    for inner, pos in ((True, place % RING), (False, place // RING)):
        ring = RING if inner else count // RING
        sent = total
        for shift in range(1, ring):
            other = lax.ppermute(sent, axis, ring_pairs(count, shift, inner))
            before = before + jnp.where(shift <= pos, other, 0.0)
            after = after + jnp.where(shift <= pos, 0.0, other)
            total = total + other
    return before, after, total


def ring_reduce_scatter(pieces, axis, inner, shift):
    count = lax.axis_size(axis)
    place = lax.axis_index(axis)
    size = pieces.shape[0] // RING
    pos = place % RING if inner else place // RING
    pairs = ring_pairs(count, shift, inner)

    def piece(index):
        return lax.dynamic_slice_in_dim(pieces, (index % RING) * size, size, 0).astype(jnp.float32)

    acc = piece(pos - shift)
    for step in range(RING - 1):
        got = lax.ppermute(acc.astype(jnp.bfloat16), axis, pairs)
        acc = got.astype(jnp.float32) + piece(pos - (2 + step) * shift)
    return acc


def grid_reduce_scatter(partial, axis, inner_first, shift):
    partial = ring_reduce_scatter(partial, axis, inner_first, shift)
    return ring_reduce_scatter(partial.astype(jnp.bfloat16), axis, not inner_first, shift)


def body(tokens, w_query, w_key, w_value, w_out, state_in, grad_out):
    head_count = state_in.shape[0]
    head_width = state_in.shape[1]
    rows_all = lax.all_gather(tokens, "tp", axis=0, tiled=True)
    shard_len = rows_all.shape[0]

    def head_split(matrix):
        return matrix.reshape(shard_len, head_count, head_width)

    query = jnp.dot(rows_all, w_query, preferred_element_type=jnp.float32).astype(jnp.bfloat16)
    key_all = jnp.dot(rows_all, w_key, preferred_element_type=jnp.float32).astype(jnp.bfloat16)
    value_all = jnp.dot(rows_all, w_value, preferred_element_type=jnp.float32).astype(jnp.bfloat16)
    query_heads = head_split(query)
    key_heads = head_split(key_all)
    value_heads = head_split(value_all)
    query_full = query_heads.astype(jnp.float32)
    key_full = key_heads.astype(jnp.float32)
    value_full = value_heads.astype(jnp.float32)
    local_kv = jnp.einsum(
        "thd,the->hde", key_heads, value_heads, preferred_element_type=jnp.float32
    )
    earlier, _, _ = scanned(local_kv, "seq")
    state_before = state_in + earlier
    row_ids = lax.broadcasted_iota(jnp.int32, (shard_len, shard_len), 0)
    col_ids = lax.broadcasted_iota(jnp.int32, (shard_len, shard_len), 1)
    mask = (row_ids >= col_ids)[None]
    scores = jnp.einsum("thd,shd->hts", query_heads, key_heads, preferred_element_type=jnp.float32)
    masked = jnp.where(mask, scores, 0.0)
    attn = jnp.einsum("hts,shd->thd", masked, value_full, precision=HIGH) + jnp.einsum(
        "thd,hde->the", query_full, state_before, precision=HIGH
    )
    inverse = lax.rsqrt(jnp.mean(attn * attn, axis=-1, keepdims=True) + 1e-05)
    normed = attn * inverse
    heads_out = normed.reshape(shard_len, head_count * head_width).astype(jnp.bfloat16)
    mixed_out = lax.psum_scatter(
        jnp.dot(heads_out, w_out, preferred_element_type=jnp.float32).astype(jnp.bfloat16),
        "tp",
        scatter_dimension=0,
        tiled=True,
    )
    grad_all = lax.all_gather(grad_out, "tp", axis=0, tiled=True)
    d_normed = lax.dot_general(grad_all, w_out, COLS_CONTRACT, preferred_element_type=jnp.float32)
    d_normed = d_normed.reshape(shard_len, head_count, head_width)
    d_attn = inverse * (d_normed - normed * jnp.mean(d_normed * normed, axis=-1, keepdims=True))
    local_adj = jnp.einsum("thd,the->hde", query_full, d_attn, precision=HIGH)
    _, later, adj_total = scanned(local_adj, "seq")
    rows_per = head_width // lax.axis_size("seq")
    state_grad = lax.dynamic_slice_in_dim(
        adj_total, lax.axis_index("seq") * rows_per, rows_per, axis=1
    )
    mixed_s = jnp.where(mask, jnp.einsum("the,she->hts", d_attn, value_full, precision=HIGH), 0.0)
    grad_q = jnp.einsum("the,hde->thd", d_attn, state_before, precision=HIGH) + jnp.einsum(
        "hts,shd->thd", mixed_s, key_full, precision=HIGH
    )
    grad_k = jnp.einsum("hts,thd->shd", mixed_s, query_full, precision=HIGH) + jnp.einsum(
        "hde,she->shd", later, value_full, precision=HIGH
    )
    grad_v = jnp.einsum("hts,the->she", masked, d_attn, precision=HIGH) + jnp.einsum(
        "hde,shd->she", later, key_full, precision=HIGH
    )
    query_grad = grad_q.reshape(shard_len, head_count * head_width).astype(jnp.bfloat16)
    key_grad = grad_k.reshape(shard_len, head_count * head_width).astype(jnp.bfloat16)
    value_grad = grad_v.reshape(shard_len, head_count * head_width).astype(jnp.bfloat16)
    term = lax.dot_general(query_grad, w_query, COLS_CONTRACT, preferred_element_type=jnp.float32)
    term = term + lax.dot_general(
        key_grad, w_key, COLS_CONTRACT, preferred_element_type=jnp.float32
    )
    input_grad = lax.psum_scatter(
        (
            term
            + lax.dot_general(
                value_grad, w_value, COLS_CONTRACT, preferred_element_type=jnp.float32
            )
        ).astype(jnp.bfloat16),
        "tp",
        scatter_dimension=0,
        tiled=True,
    )
    outer = lax.axis_size("seq") // RING
    rows_swapped = (
        rows_all.reshape(shard_len, outer, RING, -1)
        .transpose(0, 2, 1, 3)
        .reshape(shard_len, -1)
    )
    out_sum = grid_reduce_scatter(
        lax.dot_general(grad_all, heads_out, ROWS_CONTRACT, preferred_element_type=jnp.bfloat16),
        "seq",
        False,
        -1,
    )
    query_sum = grid_reduce_scatter(
        lax.dot_general(rows_swapped, query_grad, ROWS_CONTRACT, preferred_element_type=jnp.bfloat16),
        "seq",
        True,
        1,
    )
    key_sum = grid_reduce_scatter(
        lax.dot_general(rows_swapped, key_grad, ROWS_CONTRACT, preferred_element_type=jnp.bfloat16),
        "seq",
        True,
        -1,
    )
    value_sum = grid_reduce_scatter(
        lax.dot_general(rows_all, value_grad, ROWS_CONTRACT, preferred_element_type=jnp.bfloat16),
        "seq",
        False,
        1,
    )
    out_summed = out_sum.T
    grad_scale = lax.rsqrt(jnp.float32(shard_len * lax.axis_size("seq")))
    return (
        mixed_out,
        input_grad,
        query_sum.astype(jnp.float32) * grad_scale,
        key_sum.astype(jnp.float32) * grad_scale,
        value_sum.astype(jnp.float32) * grad_scale,
        out_summed.astype(jnp.float32) * grad_scale,
        state_grad,
    )


def solution(mesh):
    return jax.shard_map(
        body,
        mesh=mesh,
        in_specs=(
            P(("seq", "tp"), None),
            P(None, "tp"),
            P(None, "tp"),
            P(None, "tp"),
            P("tp", None),
            P("tp", None, None),
            P(("seq", "tp"), None),
        ),
        out_specs=(
            P(("seq", "tp"), None),
            P(("seq", "tp"), None),
            P("seq", "tp"),
            P("seq", "tp"),
            P("seq", "tp"),
            P("tp", "seq"),
            P("tp", "seq", None),
        ),
        check_vma=False,
    )
```

```python
import jax
import jax.numpy as jnp
from jax import lax
from jax.sharding import PartitionSpec as P

HIGH = lax.Precision.HIGHEST
ROWS_CONTRACT = (((0,), (0,)), ((), ()))
COLS_CONTRACT = (((1,), (1,)), ((), ()))


def scanned(array, axis):
    count = lax.axis_size(axis)
    place = lax.axis_index(axis)
    total = array
    before = jnp.zeros_like(array)
    after = jnp.zeros_like(array)
    step = 1
    while step < count:
        pairs = [(i, i ^ step) for i in range(count)]
        other = lax.ppermute(total, axis, pairs)
        upper = (place & step) != 0
        before = before + jnp.where(upper, other, 0.0)
        after = after + jnp.where(upper, 0.0, other)
        total = total + other
        step *= 2
    return before, after, total


RING = 4


def ring_pairs(count, shift, inner):
    pairs = []
    for place in range(count):
        outer, within = divmod(place, RING)
        if inner:
            target = outer * RING + (within + shift) % RING
        else:
            target = ((outer + shift) % (count // RING)) * RING + within
        pairs.append((place, target))
    return pairs


def ring_reduce_scatter(pieces, axis, inner, shift):
    count = lax.axis_size(axis)
    place = lax.axis_index(axis)
    size = pieces.shape[0] // RING
    pos = place % RING if inner else place // RING
    pairs = ring_pairs(count, shift, inner)

    def piece(index):
        return lax.dynamic_slice_in_dim(pieces, (index % RING) * size, size, 0).astype(jnp.float32)

    acc = piece(pos - shift)
    for step in range(RING - 1):
        got = lax.ppermute(acc.astype(jnp.bfloat16), axis, pairs)
        acc = got.astype(jnp.float32) + piece(pos - (2 + step) * shift)
    return acc


def grid_reduce_scatter(partial, axis, inner_first, shift):
    partial = ring_reduce_scatter(partial, axis, inner_first, shift)
    return ring_reduce_scatter(partial.astype(jnp.bfloat16), axis, not inner_first, shift)


def body(tokens, w_query, w_key, w_value, w_out, state_in, grad_out):
    head_count = state_in.shape[0]
    head_width = state_in.shape[1]
    rows_all = lax.all_gather(tokens, "tp", axis=0, tiled=True)
    shard_len = rows_all.shape[0]

    def head_split(matrix):
        return matrix.reshape(shard_len, head_count, head_width)

    query = jnp.dot(rows_all, w_query, preferred_element_type=jnp.float32).astype(jnp.bfloat16)
    key_all = jnp.dot(rows_all, w_key, preferred_element_type=jnp.float32).astype(jnp.bfloat16)
    value_all = jnp.dot(rows_all, w_value, preferred_element_type=jnp.float32).astype(jnp.bfloat16)
    query_heads = head_split(query)
    key_heads = head_split(key_all)
    value_heads = head_split(value_all)
    query_full = query_heads.astype(jnp.float32)
    key_full = key_heads.astype(jnp.float32)
    value_full = value_heads.astype(jnp.float32)
    local_kv = jnp.einsum(
        "thd,the->hde", key_heads, value_heads, preferred_element_type=jnp.float32
    )
    earlier, _, _ = scanned(local_kv, "seq")
    state_before = state_in + earlier
    row_ids = lax.broadcasted_iota(jnp.int32, (shard_len, shard_len), 0)
    col_ids = lax.broadcasted_iota(jnp.int32, (shard_len, shard_len), 1)
    mask = (row_ids >= col_ids)[None]
    scores = jnp.einsum("thd,shd->hts", query_heads, key_heads, preferred_element_type=jnp.float32)
    masked = jnp.where(mask, scores, 0.0)
    attn = jnp.einsum("hts,shd->thd", masked, value_full, precision=HIGH) + jnp.einsum(
        "thd,hde->the", query_full, state_before, precision=HIGH
    )
    inverse = lax.rsqrt(jnp.mean(attn * attn, axis=-1, keepdims=True) + 1e-05)
    normed = attn * inverse
    heads_out = normed.reshape(shard_len, head_count * head_width).astype(jnp.bfloat16)
    mixed_out = lax.psum_scatter(
        jnp.dot(heads_out, w_out, preferred_element_type=jnp.float32).astype(jnp.bfloat16),
        "tp",
        scatter_dimension=0,
        tiled=True,
    )
    grad_all = lax.all_gather(grad_out, "tp", axis=0, tiled=True)
    d_normed = lax.dot_general(grad_all, w_out, COLS_CONTRACT, preferred_element_type=jnp.float32)
    d_normed = d_normed.reshape(shard_len, head_count, head_width)
    d_attn = inverse * (d_normed - normed * jnp.mean(d_normed * normed, axis=-1, keepdims=True))
    local_adj = jnp.einsum("thd,the->hde", query_full, d_attn, precision=HIGH)
    _, later, adj_total = scanned(local_adj, "seq")
    rows_per = head_width // lax.axis_size("seq")
    state_grad = lax.dynamic_slice_in_dim(
        adj_total, lax.axis_index("seq") * rows_per, rows_per, axis=1
    )
    mixed_s = jnp.where(mask, jnp.einsum("the,she->hts", d_attn, value_full, precision=HIGH), 0.0)
    grad_q = jnp.einsum("the,hde->thd", d_attn, state_before, precision=HIGH) + jnp.einsum(
        "hts,shd->thd", mixed_s, key_full, precision=HIGH
    )
    grad_k = jnp.einsum("hts,thd->shd", mixed_s, query_full, precision=HIGH) + jnp.einsum(
        "hde,she->shd", later, value_full, precision=HIGH
    )
    grad_v = jnp.einsum("hts,the->she", masked, d_attn, precision=HIGH) + jnp.einsum(
        "hde,shd->she", later, key_full, precision=HIGH
    )
    query_grad = grad_q.reshape(shard_len, head_count * head_width).astype(jnp.bfloat16)
    key_grad = grad_k.reshape(shard_len, head_count * head_width).astype(jnp.bfloat16)
    value_grad = grad_v.reshape(shard_len, head_count * head_width).astype(jnp.bfloat16)
    term = lax.dot_general(query_grad, w_query, COLS_CONTRACT, preferred_element_type=jnp.float32)
    term = term + lax.dot_general(
        key_grad, w_key, COLS_CONTRACT, preferred_element_type=jnp.float32
    )
    input_grad = lax.psum_scatter(
        (
            term
            + lax.dot_general(
                value_grad, w_value, COLS_CONTRACT, preferred_element_type=jnp.float32
            )
        ).astype(jnp.bfloat16),
        "tp",
        scatter_dimension=0,
        tiled=True,
    )
    outer = lax.axis_size("seq") // RING
    rows_swapped = (
        rows_all.reshape(shard_len, outer, RING, -1)
        .transpose(0, 2, 1, 3)
        .reshape(shard_len, -1)
    )
    out_sum = grid_reduce_scatter(
        lax.dot_general(grad_all, heads_out, ROWS_CONTRACT, preferred_element_type=jnp.bfloat16),
        "seq",
        False,
        -1,
    )
    routes = ((True, 1), (True, -1), (False, 1), (False, -1))
    quarter = query_grad.shape[1] // len(routes)
    sums = []
    for index, (inner_first, shift) in enumerate(routes):
        cols = slice(index * quarter, (index + 1) * quarter)
        grads = jnp.concatenate([query_grad[:, cols], key_grad[:, cols], value_grad[:, cols]], axis=1)
        sums.append(
            grid_reduce_scatter(
                lax.dot_general(
                    rows_swapped if inner_first else rows_all,
                    grads,
                    ROWS_CONTRACT,
                    preferred_element_type=jnp.bfloat16,
                ),
                "seq",
                inner_first,
                shift,
            )
        )
    query_sum, key_sum, value_sum = (
        jnp.concatenate([part[:, k * quarter : (k + 1) * quarter] for part in sums], axis=1)
        for k in range(3)
    )
    out_summed = out_sum.T
    grad_scale = lax.rsqrt(jnp.float32(shard_len * lax.axis_size("seq")))
    return (
        mixed_out,
        input_grad,
        query_sum.astype(jnp.float32) * grad_scale,
        key_sum.astype(jnp.float32) * grad_scale,
        value_sum.astype(jnp.float32) * grad_scale,
        out_summed.astype(jnp.float32) * grad_scale,
        state_grad,
    )


def solution(mesh):
    return jax.shard_map(
        body,
        mesh=mesh,
        in_specs=(
            P(("seq", "tp"), None),
            P(None, "tp"),
            P(None, "tp"),
            P(None, "tp"),
            P("tp", None),
            P("tp", None, None),
            P(("seq", "tp"), None),
        ),
        out_specs=(
            P(("seq", "tp"), None),
            P(("seq", "tp"), None),
            P("seq", "tp"),
            P("seq", "tp"),
            P("seq", "tp"),
            P("tp", "seq"),
            P("tp", "seq", None),
        ),
        check_vma=False,
    )
```

```python
import jax
import jax.numpy as jnp
from jax import lax
from jax.sharding import PartitionSpec as P

HIGH = lax.Precision.HIGHEST
ROWS_CONTRACT = (((0,), (0,)), ((), ()))
COLS_CONTRACT = (((1,), (1,)), ((), ()))


def scanned(array, axis):
    count = lax.axis_size(axis)
    place = lax.axis_index(axis)
    total = array
    before = jnp.zeros_like(array)
    after = jnp.zeros_like(array)
    step = 1
    while step < count:
        pairs = [(i, i ^ step) for i in range(count)]
        other = lax.ppermute(total.astype(jnp.bfloat16), axis, pairs).astype(jnp.float32)
        upper = (place & step) != 0
        before = before + jnp.where(upper, other, 0.0)
        after = after + jnp.where(upper, 0.0, other)
        total = total + other
        step *= 2
    return before, after, total


RING = 4


def ring_pairs(count, shift, inner):
    pairs = []
    for place in range(count):
        outer, within = divmod(place, RING)
        if inner:
            target = outer * RING + (within + shift) % RING
        else:
            target = ((outer + shift) % (count // RING)) * RING + within
        pairs.append((place, target))
    return pairs


def ring_reduce_scatter(pieces, axis, inner, shift):
    count = lax.axis_size(axis)
    place = lax.axis_index(axis)
    size = pieces.shape[0] // RING
    pos = place % RING if inner else place // RING
    pairs = ring_pairs(count, shift, inner)

    def piece(index):
        return lax.dynamic_slice_in_dim(pieces, (index % RING) * size, size, 0).astype(jnp.float32)

    acc = piece(pos - shift)
    for step in range(RING - 1):
        got = lax.ppermute(acc.astype(jnp.bfloat16), axis, pairs)
        acc = got.astype(jnp.float32) + piece(pos - (2 + step) * shift)
    return acc


def grid_reduce_scatter(partial, axis, inner_first, shift):
    partial = ring_reduce_scatter(partial, axis, inner_first, shift)
    return ring_reduce_scatter(partial.astype(jnp.bfloat16), axis, not inner_first, shift)


def body(tokens, w_query, w_key, w_value, w_out, state_in, grad_out):
    head_count = state_in.shape[0]
    head_width = state_in.shape[1]
    rows_all = lax.all_gather(tokens, "tp", axis=0, tiled=True)
    shard_len = rows_all.shape[0]

    def head_split(matrix):
        return matrix.reshape(shard_len, head_count, head_width)

    query = jnp.dot(rows_all, w_query, preferred_element_type=jnp.float32).astype(jnp.bfloat16)
    key_all = jnp.dot(rows_all, w_key, preferred_element_type=jnp.float32).astype(jnp.bfloat16)
    value_all = jnp.dot(rows_all, w_value, preferred_element_type=jnp.float32).astype(jnp.bfloat16)
    query_heads = head_split(query)
    key_heads = head_split(key_all)
    value_heads = head_split(value_all)
    query_full = query_heads.astype(jnp.float32)
    key_full = key_heads.astype(jnp.float32)
    value_full = value_heads.astype(jnp.float32)
    local_kv = jnp.einsum(
        "thd,the->hde", key_heads, value_heads, preferred_element_type=jnp.float32
    )
    earlier, _, _ = scanned(local_kv, "seq")
    state_before = state_in + earlier
    row_ids = lax.broadcasted_iota(jnp.int32, (shard_len, shard_len), 0)
    col_ids = lax.broadcasted_iota(jnp.int32, (shard_len, shard_len), 1)
    mask = (row_ids >= col_ids)[None]
    scores = jnp.einsum("thd,shd->hts", query_heads, key_heads, preferred_element_type=jnp.float32)
    masked = jnp.where(mask, scores, 0.0)
    attn = jnp.einsum("hts,shd->thd", masked, value_full, precision=HIGH) + jnp.einsum(
        "thd,hde->the", query_full, state_before, precision=HIGH
    )
    inverse = lax.rsqrt(jnp.mean(attn * attn, axis=-1, keepdims=True) + 1e-05)
    normed = attn * inverse
    heads_out = normed.reshape(shard_len, head_count * head_width).astype(jnp.bfloat16)
    mixed_out = lax.psum_scatter(
        jnp.dot(heads_out, w_out, preferred_element_type=jnp.float32).astype(jnp.bfloat16),
        "tp",
        scatter_dimension=0,
        tiled=True,
    )
    grad_all = lax.all_gather(grad_out, "tp", axis=0, tiled=True)
    d_normed = lax.dot_general(grad_all, w_out, COLS_CONTRACT, preferred_element_type=jnp.float32)
    d_normed = d_normed.reshape(shard_len, head_count, head_width)
    d_attn = inverse * (d_normed - normed * jnp.mean(d_normed * normed, axis=-1, keepdims=True))
    local_adj = jnp.einsum("thd,the->hde", query_full, d_attn, precision=HIGH)
    _, later, adj_total = scanned(local_adj, "seq")
    rows_per = head_width // lax.axis_size("seq")
    state_grad = lax.dynamic_slice_in_dim(
        adj_total, lax.axis_index("seq") * rows_per, rows_per, axis=1
    )
    mixed_s = jnp.where(mask, jnp.einsum("the,she->hts", d_attn, value_full, precision=HIGH), 0.0)
    grad_q = jnp.einsum("the,hde->thd", d_attn, state_before, precision=HIGH) + jnp.einsum(
        "hts,shd->thd", mixed_s, key_full, precision=HIGH
    )
    grad_k = jnp.einsum("hts,thd->shd", mixed_s, query_full, precision=HIGH) + jnp.einsum(
        "hde,she->shd", later, value_full, precision=HIGH
    )
    grad_v = jnp.einsum("hts,the->she", masked, d_attn, precision=HIGH) + jnp.einsum(
        "hde,shd->she", later, key_full, precision=HIGH
    )
    query_grad = grad_q.reshape(shard_len, head_count * head_width).astype(jnp.bfloat16)
    key_grad = grad_k.reshape(shard_len, head_count * head_width).astype(jnp.bfloat16)
    value_grad = grad_v.reshape(shard_len, head_count * head_width).astype(jnp.bfloat16)
    term = lax.dot_general(query_grad, w_query, COLS_CONTRACT, preferred_element_type=jnp.float32)
    term = term + lax.dot_general(
        key_grad, w_key, COLS_CONTRACT, preferred_element_type=jnp.float32
    )
    input_grad = lax.psum_scatter(
        (
            term
            + lax.dot_general(
                value_grad, w_value, COLS_CONTRACT, preferred_element_type=jnp.float32
            )
        ).astype(jnp.bfloat16),
        "tp",
        scatter_dimension=0,
        tiled=True,
    )
    outer = lax.axis_size("seq") // RING
    rows_swapped = (
        rows_all.reshape(shard_len, outer, RING, -1)
        .transpose(0, 2, 1, 3)
        .reshape(shard_len, -1)
    )
    out_sum = grid_reduce_scatter(
        lax.dot_general(grad_all, heads_out, ROWS_CONTRACT, preferred_element_type=jnp.bfloat16),
        "seq",
        False,
        -1,
    )
    routes = ((True, 1), (True, -1), (False, 1), (False, -1))
    quarter = query_grad.shape[1] // len(routes)
    sums = []
    for index, (inner_first, shift) in enumerate(routes):
        cols = slice(index * quarter, (index + 1) * quarter)
        grads = jnp.concatenate([query_grad[:, cols], key_grad[:, cols], value_grad[:, cols]], axis=1)
        sums.append(
            grid_reduce_scatter(
                lax.dot_general(
                    rows_swapped if inner_first else rows_all,
                    grads,
                    ROWS_CONTRACT,
                    preferred_element_type=jnp.bfloat16,
                ),
                "seq",
                inner_first,
                shift,
            )
        )
    query_sum, key_sum, value_sum = (
        jnp.concatenate([part[:, k * quarter : (k + 1) * quarter] for part in sums], axis=1)
        for k in range(3)
    )
    out_summed = out_sum.T
    grad_scale = lax.rsqrt(jnp.float32(shard_len * lax.axis_size("seq")))
    return (
        mixed_out,
        input_grad,
        query_sum.astype(jnp.float32) * grad_scale,
        key_sum.astype(jnp.float32) * grad_scale,
        value_sum.astype(jnp.float32) * grad_scale,
        out_summed.astype(jnp.float32) * grad_scale,
        state_grad,
    )


def solution(mesh):
    return jax.shard_map(
        body,
        mesh=mesh,
        in_specs=(
            P(("seq", "tp"), None),
            P(None, "tp"),
            P(None, "tp"),
            P(None, "tp"),
            P("tp", None),
            P("tp", None, None),
            P(("seq", "tp"), None),
        ),
        out_specs=(
            P(("seq", "tp"), None),
            P(("seq", "tp"), None),
            P("seq", "tp"),
            P("seq", "tp"),
            P("seq", "tp"),
            P("tp", "seq"),
            P("tp", "seq", None),
        ),
        check_vma=False,
    )
```

```python
import jax
import jax.numpy as jnp
from jax import lax
from jax.sharding import PartitionSpec as P

HIGH = lax.Precision.HIGHEST
ROWS_CONTRACT = (((0,), (0,)), ((), ()))
COLS_CONTRACT = (((1,), (1,)), ((), ()))


def scanned(array, axis):
    count = lax.axis_size(axis)
    place = lax.axis_index(axis)
    total = array
    before = jnp.zeros_like(array)
    after = jnp.zeros_like(array)
    step = 1
    while step < count:
        pairs = [(i, i ^ step) for i in range(count)]
        other = lax.ppermute(total, axis, pairs)
        upper = (place & step) != 0
        before = before + jnp.where(upper, other, 0.0)
        after = after + jnp.where(upper, 0.0, other)
        total = total + other
        step *= 2
    return before, after, total


RING = 4


def ring_pairs(count, shift, inner):
    pairs = []
    for place in range(count):
        outer, within = divmod(place, RING)
        if inner:
            target = outer * RING + (within + shift) % RING
        else:
            target = ((outer + shift) % (count // RING)) * RING + within
        pairs.append((place, target))
    return pairs


def ring_reduce_scatter(pieces, axis, inner, shift):
    count = lax.axis_size(axis)
    place = lax.axis_index(axis)
    size = pieces.shape[0] // RING
    pos = place % RING if inner else place // RING
    pairs = ring_pairs(count, shift, inner)

    def piece(index):
        return lax.dynamic_slice_in_dim(pieces, (index % RING) * size, size, 0).astype(jnp.float32)

    acc = piece(pos - shift)
    for step in range(RING - 1):
        got = lax.ppermute(acc.astype(jnp.bfloat16), axis, pairs)
        acc = got.astype(jnp.float32) + piece(pos - (2 + step) * shift)
    return acc


def grid_reduce_scatter(partial, axis, inner_first, shift):
    partial = ring_reduce_scatter(partial, axis, inner_first, shift)
    return ring_reduce_scatter(partial.astype(jnp.bfloat16), axis, not inner_first, shift)


def body(tokens, w_query, w_key, w_value, w_out, state_in, grad_out):
    head_count = state_in.shape[0]
    head_width = state_in.shape[1]
    rows_all = lax.all_gather(tokens, "tp", axis=0, tiled=True)
    shard_len = rows_all.shape[0]

    def head_split(matrix):
        return matrix.reshape(shard_len, head_count, head_width)

    query = jnp.dot(rows_all, w_query, preferred_element_type=jnp.float32).astype(jnp.bfloat16)
    key_all = jnp.dot(rows_all, w_key, preferred_element_type=jnp.float32).astype(jnp.bfloat16)
    value_all = jnp.dot(rows_all, w_value, preferred_element_type=jnp.float32).astype(jnp.bfloat16)
    query_heads = head_split(query)
    key_heads = head_split(key_all)
    value_heads = head_split(value_all)
    query_full = query_heads.astype(jnp.float32)
    key_full = key_heads.astype(jnp.float32)
    value_full = value_heads.astype(jnp.float32)
    local_kv = jnp.einsum(
        "thd,the->hde", key_heads, value_heads, preferred_element_type=jnp.float32
    )
    earlier, _, _ = scanned(local_kv, "seq")
    state_before = state_in + earlier
    row_ids = lax.broadcasted_iota(jnp.int32, (shard_len, shard_len), 0)
    col_ids = lax.broadcasted_iota(jnp.int32, (shard_len, shard_len), 1)
    mask = (row_ids >= col_ids)[None]
    scores = jnp.einsum("thd,shd->hts", query_heads, key_heads, preferred_element_type=jnp.float32)
    masked = jnp.where(mask, scores, 0.0)
    attn = jnp.einsum("hts,shd->thd", masked, value_full, precision=HIGH) + jnp.einsum(
        "thd,hde->the", query_full, state_before, precision=HIGH
    )
    inverse = lax.rsqrt(jnp.mean(attn * attn, axis=-1, keepdims=True) + 1e-05)
    normed = attn * inverse
    heads_out = normed.reshape(shard_len, head_count * head_width).astype(jnp.bfloat16)
    mixed_out = lax.psum_scatter(
        jnp.dot(heads_out, w_out, preferred_element_type=jnp.float32).astype(jnp.bfloat16),
        "tp",
        scatter_dimension=0,
        tiled=True,
    )
    grad_all = lax.all_gather(grad_out, "tp", axis=0, tiled=True)
    d_normed = lax.dot_general(grad_all, w_out, COLS_CONTRACT, preferred_element_type=jnp.float32)
    d_normed = d_normed.reshape(shard_len, head_count, head_width)
    d_attn = inverse * (d_normed - normed * jnp.mean(d_normed * normed, axis=-1, keepdims=True))
    local_adj = jnp.einsum("thd,the->hde", query_full, d_attn, precision=HIGH)
    _, later, adj_total = scanned(local_adj, "seq")
    rows_per = head_width // lax.axis_size("seq")
    state_grad = lax.dynamic_slice_in_dim(
        adj_total, lax.axis_index("seq") * rows_per, rows_per, axis=1
    )
    mixed_s = jnp.where(mask, jnp.einsum("the,she->hts", d_attn, value_full, precision=HIGH), 0.0)
    grad_q = jnp.einsum("the,hde->thd", d_attn, state_before, precision=HIGH) + jnp.einsum(
        "hts,shd->thd", mixed_s, key_full, precision=HIGH
    )
    grad_k = jnp.einsum("hts,thd->shd", mixed_s, query_full, precision=HIGH) + jnp.einsum(
        "hde,she->shd", later, value_full, precision=HIGH
    )
    grad_v = jnp.einsum("hts,the->she", masked, d_attn, precision=HIGH) + jnp.einsum(
        "hde,shd->she", later, key_full, precision=HIGH
    )
    query_grad = grad_q.reshape(shard_len, head_count * head_width).astype(jnp.bfloat16)
    key_grad = grad_k.reshape(shard_len, head_count * head_width).astype(jnp.bfloat16)
    value_grad = grad_v.reshape(shard_len, head_count * head_width).astype(jnp.bfloat16)
    term = lax.dot_general(query_grad, w_query, COLS_CONTRACT, preferred_element_type=jnp.float32)
    term = term + lax.dot_general(
        key_grad, w_key, COLS_CONTRACT, preferred_element_type=jnp.float32
    )
    input_grad = lax.psum_scatter(
        (
            term
            + lax.dot_general(
                value_grad, w_value, COLS_CONTRACT, preferred_element_type=jnp.float32
            )
        ).astype(jnp.bfloat16),
        "tp",
        scatter_dimension=0,
        tiled=True,
    )
    outer = lax.axis_size("seq") // RING
    rows_swapped = (
        rows_all.reshape(shard_len, outer, RING, -1)
        .transpose(0, 2, 1, 3)
        .reshape(shard_len, -1)
    )
    grad_swapped = (
        grad_all.reshape(shard_len, outer, RING, -1)
        .transpose(0, 2, 1, 3)
        .reshape(shard_len, -1)
    )
    routes = ((True, 1), (True, -1), (False, 1), (False, -1))
    quarter = query_grad.shape[1] // len(routes)
    sums = []
    for index, (inner_first, shift) in enumerate(routes):
        cols = slice(index * quarter, (index + 1) * quarter)
        grads = jnp.concatenate([query_grad[:, cols], key_grad[:, cols], value_grad[:, cols]], axis=1)
        partial = jnp.concatenate(
            [
                lax.dot_general(
                    rows_swapped if inner_first else rows_all,
                    grads,
                    ROWS_CONTRACT,
                    preferred_element_type=jnp.bfloat16,
                ),
                lax.dot_general(
                    grad_swapped if inner_first else grad_all,
                    heads_out[:, cols],
                    ROWS_CONTRACT,
                    preferred_element_type=jnp.bfloat16,
                ),
            ],
            axis=1,
        )
        sums.append(grid_reduce_scatter(partial, "seq", inner_first, shift))
    query_sum, key_sum, value_sum, out_sum = (
        jnp.concatenate([part[:, k * quarter : (k + 1) * quarter] for part in sums], axis=1)
        for k in range(4)
    )
    out_summed = out_sum.T
    grad_scale = lax.rsqrt(jnp.float32(shard_len * lax.axis_size("seq")))
    return (
        mixed_out,
        input_grad,
        query_sum.astype(jnp.float32) * grad_scale,
        key_sum.astype(jnp.float32) * grad_scale,
        value_sum.astype(jnp.float32) * grad_scale,
        out_summed.astype(jnp.float32) * grad_scale,
        state_grad,
    )


def solution(mesh):
    return jax.shard_map(
        body,
        mesh=mesh,
        in_specs=(
            P(("seq", "tp"), None),
            P(None, "tp"),
            P(None, "tp"),
            P(None, "tp"),
            P("tp", None),
            P("tp", None, None),
            P(("seq", "tp"), None),
        ),
        out_specs=(
            P(("seq", "tp"), None),
            P(("seq", "tp"), None),
            P("seq", "tp"),
            P("seq", "tp"),
            P("seq", "tp"),
            P("tp", "seq"),
            P("tp", "seq", None),
        ),
        check_vma=False,
    )
```

```python
import jax
import jax.numpy as jnp
from jax import lax
from jax.sharding import PartitionSpec as P

HIGH = lax.Precision.HIGHEST
ROWS_CONTRACT = (((0,), (0,)), ((), ()))
COLS_CONTRACT = (((1,), (1,)), ((), ()))


def scanned(array, axis):
    count = lax.axis_size(axis)
    place = lax.axis_index(axis)
    total = array
    before = jnp.zeros_like(array)
    after = jnp.zeros_like(array)
    step = 1
    while step < count:
        pairs = [(i, i ^ step) for i in range(count)]
        other = lax.ppermute(total, axis, pairs)
        upper = (place & step) != 0
        before = before + jnp.where(upper, other, 0.0)
        after = after + jnp.where(upper, 0.0, other)
        total = total + other
        step *= 2
    return before, after, total


RING = 4


def ring_pairs(count, shift, inner):
    pairs = []
    for place in range(count):
        outer, within = divmod(place, RING)
        if inner:
            target = outer * RING + (within + shift) % RING
        else:
            target = ((outer + shift) % (count // RING)) * RING + within
        pairs.append((place, target))
    return pairs


def ring_reduce_scatter(pieces, axis, inner, shift):
    count = lax.axis_size(axis)
    place = lax.axis_index(axis)
    size = pieces.shape[0] // RING
    pos = place % RING if inner else place // RING
    pairs = ring_pairs(count, shift, inner)

    def piece(index):
        return lax.dynamic_slice_in_dim(pieces, (index % RING) * size, size, 0).astype(jnp.float32)

    acc = piece(pos - shift)
    for step in range(RING - 1):
        got = lax.ppermute(acc.astype(jnp.bfloat16), axis, pairs)
        acc = got.astype(jnp.float32) + piece(pos - (2 + step) * shift)
    return acc


def grid_reduce_scatter(partial, axis, inner_first, shift):
    partial = ring_reduce_scatter(partial, axis, inner_first, shift)
    return ring_reduce_scatter(partial.astype(jnp.bfloat16), axis, not inner_first, shift)


def body(tokens, w_query, w_key, w_value, w_out, state_in, grad_out):
    head_count = state_in.shape[0]
    head_width = state_in.shape[1]
    rows_all = lax.all_gather(tokens, "tp", axis=0, tiled=True)
    shard_len = rows_all.shape[0]

    def head_split(matrix):
        return matrix.reshape(shard_len, head_count, head_width)

    query = jnp.dot(rows_all, w_query, preferred_element_type=jnp.float32).astype(jnp.bfloat16)
    key_all = jnp.dot(rows_all, w_key, preferred_element_type=jnp.float32).astype(jnp.bfloat16)
    value_all = jnp.dot(rows_all, w_value, preferred_element_type=jnp.float32).astype(jnp.bfloat16)
    query_heads = head_split(query)
    key_heads = head_split(key_all)
    value_heads = head_split(value_all)
    query_full = query_heads.astype(jnp.float32)
    key_full = key_heads.astype(jnp.float32)
    value_full = value_heads.astype(jnp.float32)
    local_kv = jnp.einsum(
        "thd,the->hde", key_heads, value_heads, preferred_element_type=jnp.float32
    )
    earlier, _, _ = scanned(local_kv, "seq")
    state_before = state_in + earlier
    row_ids = lax.broadcasted_iota(jnp.int32, (shard_len, shard_len), 0)
    col_ids = lax.broadcasted_iota(jnp.int32, (shard_len, shard_len), 1)
    mask = (row_ids >= col_ids)[None]
    scores = jnp.einsum("thd,shd->hts", query_heads, key_heads, preferred_element_type=jnp.float32)
    masked = jnp.where(mask, scores, 0.0)
    attn = jnp.einsum("hts,shd->thd", masked, value_full, precision=HIGH) + jnp.einsum(
        "thd,hde->the", query_full, state_before, precision=HIGH
    )
    inverse = lax.rsqrt(jnp.mean(attn * attn, axis=-1, keepdims=True) + 1e-05)
    normed = attn * inverse
    heads_out = normed.reshape(shard_len, head_count * head_width).astype(jnp.bfloat16)
    mixed_out = lax.psum_scatter(
        jnp.dot(heads_out, w_out, preferred_element_type=jnp.float32).astype(jnp.bfloat16),
        "tp",
        scatter_dimension=0,
        tiled=True,
    )
    grad_all = lax.all_gather(grad_out, "tp", axis=0, tiled=True)
    d_normed = lax.dot_general(grad_all, w_out, COLS_CONTRACT, preferred_element_type=jnp.float32)
    d_normed = d_normed.reshape(shard_len, head_count, head_width)
    d_attn = inverse * (d_normed - normed * jnp.mean(d_normed * normed, axis=-1, keepdims=True))
    local_adj = jnp.einsum("thd,the->hde", query_full, d_attn, precision=HIGH)
    _, later, adj_total = scanned(local_adj, "seq")
    rows_per = head_width // lax.axis_size("seq")
    state_grad = lax.dynamic_slice_in_dim(
        adj_total, lax.axis_index("seq") * rows_per, rows_per, axis=1
    )
    mixed_s = jnp.where(mask, jnp.einsum("the,she->hts", d_attn, value_full, precision=HIGH), 0.0)
    grad_q = jnp.einsum("the,hde->thd", d_attn, state_before, precision=HIGH) + jnp.einsum(
        "hts,shd->thd", mixed_s, key_full, precision=HIGH
    )
    grad_k = jnp.einsum("hts,thd->shd", mixed_s, query_full, precision=HIGH) + jnp.einsum(
        "hde,she->shd", later, value_full, precision=HIGH
    )
    grad_v = jnp.einsum("hts,the->she", masked, d_attn, precision=HIGH) + jnp.einsum(
        "hde,shd->she", later, key_full, precision=HIGH
    )
    query_grad = grad_q.reshape(shard_len, head_count * head_width).astype(jnp.bfloat16)
    key_grad = grad_k.reshape(shard_len, head_count * head_width).astype(jnp.bfloat16)
    value_grad = grad_v.reshape(shard_len, head_count * head_width).astype(jnp.bfloat16)
    term = lax.dot_general(query_grad, w_query, COLS_CONTRACT, preferred_element_type=jnp.float32)
    term = term + lax.dot_general(
        key_grad, w_key, COLS_CONTRACT, preferred_element_type=jnp.float32
    )
    input_grad = lax.psum_scatter(
        (
            term
            + lax.dot_general(
                value_grad, w_value, COLS_CONTRACT, preferred_element_type=jnp.float32
            )
        ).astype(jnp.bfloat16),
        "tp",
        scatter_dimension=0,
        tiled=True,
    )
    outer = lax.axis_size("seq") // RING
    rows_swapped = (
        rows_all.reshape(shard_len, outer, RING, -1)
        .transpose(0, 2, 1, 3)
        .reshape(shard_len, -1)
    )
    out_sum = grid_reduce_scatter(
        lax.dot_general(grad_all, heads_out, ROWS_CONTRACT, preferred_element_type=jnp.bfloat16),
        "seq",
        False,
        -1,
    )
    query_sum = grid_reduce_scatter(
        lax.dot_general(rows_all, query_grad, ROWS_CONTRACT, preferred_element_type=jnp.bfloat16),
        "seq",
        False,
        1,
    )
    routes = ((True, 1), (True, -1), (False, 1), (False, -1))
    quarter = key_grad.shape[1] // len(routes)
    sums = []
    for index, (inner_first, shift) in enumerate(routes):
        cols = slice(index * quarter, (index + 1) * quarter)
        grads = jnp.concatenate([key_grad[:, cols], value_grad[:, cols]], axis=1)
        sums.append(
            grid_reduce_scatter(
                lax.dot_general(
                    rows_swapped if inner_first else rows_all,
                    grads,
                    ROWS_CONTRACT,
                    preferred_element_type=jnp.bfloat16,
                ),
                "seq",
                inner_first,
                shift,
            )
        )
    key_sum, value_sum = (
        jnp.concatenate([part[:, k * quarter : (k + 1) * quarter] for part in sums], axis=1)
        for k in range(2)
    )
    out_summed = out_sum.T
    grad_scale = lax.rsqrt(jnp.float32(shard_len * lax.axis_size("seq")))
    return (
        mixed_out,
        input_grad,
        query_sum.astype(jnp.float32) * grad_scale,
        key_sum.astype(jnp.float32) * grad_scale,
        value_sum.astype(jnp.float32) * grad_scale,
        out_summed.astype(jnp.float32) * grad_scale,
        state_grad,
    )


def solution(mesh):
    return jax.shard_map(
        body,
        mesh=mesh,
        in_specs=(
            P(("seq", "tp"), None),
            P(None, "tp"),
            P(None, "tp"),
            P(None, "tp"),
            P("tp", None),
            P("tp", None, None),
            P(("seq", "tp"), None),
        ),
        out_specs=(
            P(("seq", "tp"), None),
            P(("seq", "tp"), None),
            P("seq", "tp"),
            P("seq", "tp"),
            P("seq", "tp"),
            P("tp", "seq"),
            P("tp", "seq", None),
        ),
        check_vma=False,
    )
```

```python
import jax
import jax.numpy as jnp
from jax import lax
from jax.sharding import PartitionSpec as P

HIGH = lax.Precision.HIGHEST
ROWS_CONTRACT = (((0,), (0,)), ((), ()))
COLS_CONTRACT = (((1,), (1,)), ((), ()))


def scanned(array, axis):
    count = lax.axis_size(axis)
    place = lax.axis_index(axis)
    total = array
    before = jnp.zeros_like(array)
    after = jnp.zeros_like(array)
    step = 1
    while step < count:
        pairs = [(i, i ^ step) for i in range(count)]
        other = lax.ppermute(total, axis, pairs)
        upper = (place & step) != 0
        before = before + jnp.where(upper, other, 0.0)
        after = after + jnp.where(upper, 0.0, other)
        total = total + other
        step *= 2
    return before, after, total


RING = 4


def ring_pairs(count, shift, inner):
    pairs = []
    for place in range(count):
        outer, within = divmod(place, RING)
        if inner:
            target = outer * RING + (within + shift) % RING
        else:
            target = ((outer + shift) % (count // RING)) * RING + within
        pairs.append((place, target))
    return pairs


def ring_reduce_scatter(pieces, axis, inner, shift, strided):
    count = lax.axis_size(axis)
    place = lax.axis_index(axis)
    outer = count // RING
    ring = RING if inner else outer
    pos = place % RING if inner else place // RING
    pairs = ring_pairs(count, shift, inner)
    size = pieces.shape[1] // ring

    def piece(index):
        index = index % ring
        if strided:
            block = size // outer
            chunks = [
                lax.dynamic_slice_in_dim(pieces, group * size + index * block, block, 1)
                for group in range(outer)
            ]
            return jnp.concatenate(chunks, axis=1).astype(jnp.float32)
        return lax.dynamic_slice_in_dim(pieces, index * size, size, 1).astype(jnp.float32)

    acc = piece(pos - shift)
    for step in range(ring - 1):
        got = lax.ppermute(acc.astype(jnp.bfloat16), axis, pairs)
        acc = got.astype(jnp.float32) + piece(pos - (2 + step) * shift)
    return acc


def grid_reduce_scatter(partial, axis, inner_first, shift):
    partial = ring_reduce_scatter(partial, axis, inner_first, shift, inner_first)
    return ring_reduce_scatter(partial.astype(jnp.bfloat16), axis, not inner_first, shift, False)


def body(tokens, w_query, w_key, w_value, w_out, state_in, grad_out):
    head_count = state_in.shape[0]
    head_width = state_in.shape[1]
    rows_all = lax.all_gather(tokens, "tp", axis=0, tiled=True)
    shard_len = rows_all.shape[0]

    def head_split(matrix):
        return matrix.reshape(shard_len, head_count, head_width)

    query = jnp.dot(rows_all, w_query, preferred_element_type=jnp.float32).astype(jnp.bfloat16)
    key_all = jnp.dot(rows_all, w_key, preferred_element_type=jnp.float32).astype(jnp.bfloat16)
    value_all = jnp.dot(rows_all, w_value, preferred_element_type=jnp.float32).astype(jnp.bfloat16)
    query_heads = head_split(query)
    key_heads = head_split(key_all)
    value_heads = head_split(value_all)
    query_full = query_heads.astype(jnp.float32)
    key_full = key_heads.astype(jnp.float32)
    value_full = value_heads.astype(jnp.float32)
    local_kv = jnp.einsum(
        "thd,the->hde", key_heads, value_heads, preferred_element_type=jnp.float32
    )
    earlier, _, _ = scanned(local_kv, "seq")
    state_before = state_in + earlier
    row_ids = lax.broadcasted_iota(jnp.int32, (shard_len, shard_len), 0)
    col_ids = lax.broadcasted_iota(jnp.int32, (shard_len, shard_len), 1)
    mask = (row_ids >= col_ids)[None]
    scores = jnp.einsum("thd,shd->hts", query_heads, key_heads, preferred_element_type=jnp.float32)
    masked = jnp.where(mask, scores, 0.0)
    attn = jnp.einsum("hts,shd->thd", masked, value_full, precision=HIGH) + jnp.einsum(
        "thd,hde->the", query_full, state_before, precision=HIGH
    )
    inverse = lax.rsqrt(jnp.mean(attn * attn, axis=-1, keepdims=True) + 1e-05)
    normed = attn * inverse
    heads_out = normed.reshape(shard_len, head_count * head_width).astype(jnp.bfloat16)
    mixed_out = lax.psum_scatter(
        jnp.dot(heads_out, w_out, preferred_element_type=jnp.float32).astype(jnp.bfloat16),
        "tp",
        scatter_dimension=0,
        tiled=True,
    )
    grad_all = lax.all_gather(grad_out, "tp", axis=0, tiled=True)
    d_normed = lax.dot_general(grad_all, w_out, COLS_CONTRACT, preferred_element_type=jnp.float32)
    d_normed = d_normed.reshape(shard_len, head_count, head_width)
    d_attn = inverse * (d_normed - normed * jnp.mean(d_normed * normed, axis=-1, keepdims=True))
    local_adj = jnp.einsum("thd,the->hde", query_full, d_attn, precision=HIGH)
    _, later, adj_total = scanned(local_adj, "seq")
    rows_per = head_width // lax.axis_size("seq")
    state_grad = lax.dynamic_slice_in_dim(
        adj_total, lax.axis_index("seq") * rows_per, rows_per, axis=1
    )
    mixed_s = jnp.where(mask, jnp.einsum("the,she->hts", d_attn, value_full, precision=HIGH), 0.0)
    grad_q = jnp.einsum("the,hde->thd", d_attn, state_before, precision=HIGH) + jnp.einsum(
        "hts,shd->thd", mixed_s, key_full, precision=HIGH
    )
    grad_k = jnp.einsum("hts,thd->shd", mixed_s, query_full, precision=HIGH) + jnp.einsum(
        "hde,she->shd", later, value_full, precision=HIGH
    )
    grad_v = jnp.einsum("hts,the->she", masked, d_attn, precision=HIGH) + jnp.einsum(
        "hde,shd->she", later, key_full, precision=HIGH
    )
    query_grad = grad_q.reshape(shard_len, head_count * head_width).astype(jnp.bfloat16)
    key_grad = grad_k.reshape(shard_len, head_count * head_width).astype(jnp.bfloat16)
    value_grad = grad_v.reshape(shard_len, head_count * head_width).astype(jnp.bfloat16)
    term = lax.dot_general(query_grad, w_query, COLS_CONTRACT, preferred_element_type=jnp.float32)
    term = term + lax.dot_general(
        key_grad, w_key, COLS_CONTRACT, preferred_element_type=jnp.float32
    )
    input_grad = lax.psum_scatter(
        (
            term
            + lax.dot_general(
                value_grad, w_value, COLS_CONTRACT, preferred_element_type=jnp.float32
            )
        ).astype(jnp.bfloat16),
        "tp",
        scatter_dimension=0,
        tiled=True,
    )
    out_sum = grid_reduce_scatter(
        lax.dot_general(heads_out, grad_all, ROWS_CONTRACT, preferred_element_type=jnp.bfloat16),
        "seq",
        False,
        -1,
    )
    routes = ((True, 1), (True, -1), (False, 1), (False, -1))
    quarter = query_grad.shape[1] // len(routes)
    sums = []
    for index, (inner_first, shift) in enumerate(routes):
        cols = slice(index * quarter, (index + 1) * quarter)
        grads = jnp.concatenate([query_grad[:, cols], key_grad[:, cols], value_grad[:, cols]], axis=1)
        sums.append(
            grid_reduce_scatter(
                lax.dot_general(grads, rows_all, ROWS_CONTRACT, preferred_element_type=jnp.bfloat16),
                "seq",
                inner_first,
                shift,
            )
        )
    query_sum, key_sum, value_sum = (
        jnp.concatenate([part[k * quarter : (k + 1) * quarter] for part in sums], axis=0).T
        for k in range(3)
    )
    out_summed = out_sum
    grad_scale = lax.rsqrt(jnp.float32(shard_len * lax.axis_size("seq")))
    return (
        mixed_out,
        input_grad,
        query_sum.astype(jnp.float32) * grad_scale,
        key_sum.astype(jnp.float32) * grad_scale,
        value_sum.astype(jnp.float32) * grad_scale,
        out_summed.astype(jnp.float32) * grad_scale,
        state_grad,
    )


def solution(mesh):
    return jax.shard_map(
        body,
        mesh=mesh,
        in_specs=(
            P(("seq", "tp"), None),
            P(None, "tp"),
            P(None, "tp"),
            P(None, "tp"),
            P("tp", None),
            P("tp", None, None),
            P(("seq", "tp"), None),
        ),
        out_specs=(
            P(("seq", "tp"), None),
            P(("seq", "tp"), None),
            P("seq", "tp"),
            P("seq", "tp"),
            P("seq", "tp"),
            P("tp", "seq"),
            P("tp", "seq", None),
        ),
        check_vma=False,
    )
```

```python
import jax
import jax.numpy as jnp
from jax import lax
from jax.sharding import PartitionSpec as P

HIGH = lax.Precision.HIGHEST
ROWS_CONTRACT = (((0,), (0,)), ((), ()))
COLS_CONTRACT = (((1,), (1,)), ((), ()))


def scanned(array, axis):
    count = lax.axis_size(axis)
    place = lax.axis_index(axis)
    total = array
    before = jnp.zeros_like(array)
    after = jnp.zeros_like(array)
    step = 1
    while step < count:
        pairs = [(i, i ^ step) for i in range(count)]
        other = lax.ppermute(total, axis, pairs)
        upper = (place & step) != 0
        before = before + jnp.where(upper, other, 0.0)
        after = after + jnp.where(upper, 0.0, other)
        total = total + other
        step *= 2
    return before, after, total


RING = 4


def ring_pairs(count, shift, inner):
    pairs = []
    for place in range(count):
        outer, within = divmod(place, RING)
        if inner:
            target = outer * RING + (within + shift) % RING
        else:
            target = ((outer + shift) % (count // RING)) * RING + within
        pairs.append((place, target))
    return pairs


def ring_reduce_scatter(pieces, axis, inner, shift, strided):
    count = lax.axis_size(axis)
    place = lax.axis_index(axis)
    outer = count // RING
    ring = RING if inner else outer
    pos = place % RING if inner else place // RING
    pairs = ring_pairs(count, shift, inner)
    size = pieces.shape[1] // ring

    def piece(index):
        index = index % ring
        if strided:
            block = size // outer
            chunks = [
                lax.dynamic_slice_in_dim(pieces, group * size + index * block, block, 1)
                for group in range(outer)
            ]
            return jnp.concatenate(chunks, axis=1).astype(jnp.float32)
        return lax.dynamic_slice_in_dim(pieces, index * size, size, 1).astype(jnp.float32)

    acc = piece(pos - shift)
    for step in range(ring - 1):
        got = lax.ppermute(acc.astype(jnp.bfloat16), axis, pairs)
        acc = got.astype(jnp.float32) + piece(pos - (2 + step) * shift)
    return acc


def grid_reduce_scatter(partial, axis, inner_first, shift):
    partial = ring_reduce_scatter(partial, axis, inner_first, shift, inner_first)
    return ring_reduce_scatter(partial.astype(jnp.bfloat16), axis, not inner_first, shift, False)


def body(tokens, w_query, w_key, w_value, w_out, state_in, grad_out):
    head_count = state_in.shape[0]
    head_width = state_in.shape[1]
    rows_all = lax.all_gather(tokens, "tp", axis=0, tiled=True)
    shard_len = rows_all.shape[0]

    def head_split(matrix):
        return matrix.reshape(shard_len, head_count, head_width)

    query = jnp.dot(rows_all, w_query, preferred_element_type=jnp.float32).astype(jnp.bfloat16)
    key_all = jnp.dot(rows_all, w_key, preferred_element_type=jnp.float32).astype(jnp.bfloat16)
    value_all = jnp.dot(rows_all, w_value, preferred_element_type=jnp.float32).astype(jnp.bfloat16)
    query_heads = head_split(query)
    key_heads = head_split(key_all)
    value_heads = head_split(value_all)
    query_full = query_heads.astype(jnp.float32)
    key_full = key_heads.astype(jnp.float32)
    value_full = value_heads.astype(jnp.float32)
    local_kv = jnp.einsum(
        "thd,the->hde", key_heads, value_heads, preferred_element_type=jnp.float32
    )
    earlier, _, _ = scanned(local_kv, "seq")
    state_before = state_in + earlier
    row_ids = lax.broadcasted_iota(jnp.int32, (shard_len, shard_len), 0)
    col_ids = lax.broadcasted_iota(jnp.int32, (shard_len, shard_len), 1)
    mask = (row_ids >= col_ids)[None]
    scores = jnp.einsum("thd,shd->hts", query_heads, key_heads, preferred_element_type=jnp.float32)
    masked = jnp.where(mask, scores, 0.0)
    attn = jnp.einsum("hts,shd->thd", masked, value_full, precision=HIGH) + jnp.einsum(
        "thd,hde->the", query_full, state_before, precision=HIGH
    )
    inverse = lax.rsqrt(jnp.mean(attn * attn, axis=-1, keepdims=True) + 1e-05)
    normed = attn * inverse
    heads_out = normed.reshape(shard_len, head_count * head_width).astype(jnp.bfloat16)
    mixed_out = lax.psum_scatter(
        jnp.dot(heads_out, w_out, preferred_element_type=jnp.float32).astype(jnp.bfloat16),
        "tp",
        scatter_dimension=0,
        tiled=True,
    )
    grad_all = lax.all_gather(grad_out, "tp", axis=0, tiled=True)
    d_normed = lax.dot_general(grad_all, w_out, COLS_CONTRACT, preferred_element_type=jnp.float32)
    d_normed = d_normed.reshape(shard_len, head_count, head_width)
    d_attn = inverse * (d_normed - normed * jnp.mean(d_normed * normed, axis=-1, keepdims=True))
    local_adj = jnp.einsum("thd,the->hde", query_full, d_attn, precision=HIGH)
    _, later, adj_total = scanned(local_adj, "seq")
    rows_per = head_width // lax.axis_size("seq")
    state_grad = lax.dynamic_slice_in_dim(
        adj_total, lax.axis_index("seq") * rows_per, rows_per, axis=1
    )
    mixed_s = jnp.where(mask, jnp.einsum("the,she->hts", d_attn, value_full, precision=HIGH), 0.0)
    grad_q = jnp.einsum("the,hde->thd", d_attn, state_before, precision=HIGH) + jnp.einsum(
        "hts,shd->thd", mixed_s, key_full, precision=HIGH
    )
    grad_k = jnp.einsum("hts,thd->shd", mixed_s, query_full, precision=HIGH) + jnp.einsum(
        "hde,she->shd", later, value_full, precision=HIGH
    )
    grad_v = jnp.einsum("hts,the->she", masked, d_attn, precision=HIGH) + jnp.einsum(
        "hde,shd->she", later, key_full, precision=HIGH
    )
    query_grad = grad_q.reshape(shard_len, head_count * head_width).astype(jnp.bfloat16)
    key_grad = grad_k.reshape(shard_len, head_count * head_width).astype(jnp.bfloat16)
    value_grad = grad_v.reshape(shard_len, head_count * head_width).astype(jnp.bfloat16)
    term = lax.dot_general(query_grad, w_query, COLS_CONTRACT, preferred_element_type=jnp.float32)
    term = term + lax.dot_general(
        key_grad, w_key, COLS_CONTRACT, preferred_element_type=jnp.float32
    )
    input_grad = lax.psum_scatter(
        (
            term
            + lax.dot_general(
                value_grad, w_value, COLS_CONTRACT, preferred_element_type=jnp.float32
            )
        ).astype(jnp.bfloat16),
        "tp",
        scatter_dimension=0,
        tiled=True,
    )
    out_sum = lax.psum_scatter(
        lax.dot_general(heads_out, grad_all, ROWS_CONTRACT, preferred_element_type=jnp.bfloat16),
        "seq",
        scatter_dimension=1,
        tiled=True,
    )
    routes = ((True, 1), (True, -1), (False, 1), (False, -1))
    quarter = query_grad.shape[1] // len(routes)
    sums = []
    for index, (inner_first, shift) in enumerate(routes):
        cols = slice(index * quarter, (index + 1) * quarter)
        grads = jnp.concatenate([query_grad[:, cols], key_grad[:, cols], value_grad[:, cols]], axis=1)
        sums.append(
            grid_reduce_scatter(
                lax.dot_general(grads, rows_all, ROWS_CONTRACT, preferred_element_type=jnp.bfloat16),
                "seq",
                inner_first,
                shift,
            )
        )
    query_sum, key_sum, value_sum = (
        jnp.concatenate([part[k * quarter : (k + 1) * quarter] for part in sums], axis=0).T
        for k in range(3)
    )
    out_summed = out_sum
    grad_scale = lax.rsqrt(jnp.float32(shard_len * lax.axis_size("seq")))
    return (
        mixed_out,
        input_grad,
        query_sum.astype(jnp.float32) * grad_scale,
        key_sum.astype(jnp.float32) * grad_scale,
        value_sum.astype(jnp.float32) * grad_scale,
        out_summed.astype(jnp.float32) * grad_scale,
        state_grad,
    )


def solution(mesh):
    return jax.shard_map(
        body,
        mesh=mesh,
        in_specs=(
            P(("seq", "tp"), None),
            P(None, "tp"),
            P(None, "tp"),
            P(None, "tp"),
            P("tp", None),
            P("tp", None, None),
            P(("seq", "tp"), None),
        ),
        out_specs=(
            P(("seq", "tp"), None),
            P(("seq", "tp"), None),
            P("seq", "tp"),
            P("seq", "tp"),
            P("seq", "tp"),
            P("tp", "seq"),
            P("tp", "seq", None),
        ),
        check_vma=False,
    )
```

```python
import jax
import jax.numpy as jnp
from jax import lax
from jax.sharding import PartitionSpec as P

HIGH = lax.Precision.HIGH
ROWS_CONTRACT = (((0,), (0,)), ((), ()))
COLS_CONTRACT = (((1,), (1,)), ((), ()))


def scanned(array, axis):
    count = lax.axis_size(axis)
    place = lax.axis_index(axis)
    total = array
    before = jnp.zeros_like(array)
    after = jnp.zeros_like(array)
    step = 1
    while step < count:
        pairs = [(i, i ^ step) for i in range(count)]
        other = lax.ppermute(total, axis, pairs)
        upper = (place & step) != 0
        before = before + jnp.where(upper, other, 0.0)
        after = after + jnp.where(upper, 0.0, other)
        total = total + other
        step *= 2
    return before, after, total


RING = 4


def ring_pairs(count, shift, inner):
    pairs = []
    for place in range(count):
        outer, within = divmod(place, RING)
        if inner:
            target = outer * RING + (within + shift) % RING
        else:
            target = ((outer + shift) % (count // RING)) * RING + within
        pairs.append((place, target))
    return pairs


def ring_reduce_scatter(pieces, axis, inner, shift, strided):
    count = lax.axis_size(axis)
    place = lax.axis_index(axis)
    outer = count // RING
    ring = RING if inner else outer
    pos = place % RING if inner else place // RING
    pairs = ring_pairs(count, shift, inner)
    size = pieces.shape[1] // ring

    def piece(index):
        index = index % ring
        if strided:
            block = size // outer
            chunks = [
                lax.dynamic_slice_in_dim(pieces, group * size + index * block, block, 1)
                for group in range(outer)
            ]
            return jnp.concatenate(chunks, axis=1).astype(jnp.float32)
        return lax.dynamic_slice_in_dim(pieces, index * size, size, 1).astype(jnp.float32)

    acc = piece(pos - shift)
    for step in range(ring - 1):
        got = lax.ppermute(acc.astype(jnp.bfloat16), axis, pairs)
        acc = got.astype(jnp.float32) + piece(pos - (2 + step) * shift)
    return acc


def grid_reduce_scatter(partial, axis, inner_first, shift):
    partial = ring_reduce_scatter(partial, axis, inner_first, shift, inner_first)
    return ring_reduce_scatter(partial.astype(jnp.bfloat16), axis, not inner_first, shift, False)


def body(tokens, w_query, w_key, w_value, w_out, state_in, grad_out):
    head_count = state_in.shape[0]
    head_width = state_in.shape[1]
    rows_all = lax.all_gather(tokens, "tp", axis=0, tiled=True)
    shard_len = rows_all.shape[0]

    def head_split(matrix):
        return matrix.reshape(shard_len, head_count, head_width)

    query = jnp.dot(rows_all, w_query, preferred_element_type=jnp.float32).astype(jnp.bfloat16)
    key_all = jnp.dot(rows_all, w_key, preferred_element_type=jnp.float32).astype(jnp.bfloat16)
    value_all = jnp.dot(rows_all, w_value, preferred_element_type=jnp.float32).astype(jnp.bfloat16)
    query_heads = head_split(query)
    key_heads = head_split(key_all)
    value_heads = head_split(value_all)
    query_full = query_heads.astype(jnp.float32)
    key_full = key_heads.astype(jnp.float32)
    value_full = value_heads.astype(jnp.float32)
    local_kv = jnp.einsum(
        "thd,the->hde", key_heads, value_heads, preferred_element_type=jnp.float32
    )
    earlier, _, _ = scanned(local_kv, "seq")
    state_before = state_in + earlier
    row_ids = lax.broadcasted_iota(jnp.int32, (shard_len, shard_len), 0)
    col_ids = lax.broadcasted_iota(jnp.int32, (shard_len, shard_len), 1)
    mask = (row_ids >= col_ids)[None]
    scores = jnp.einsum("thd,shd->hts", query_heads, key_heads, preferred_element_type=jnp.float32)
    masked = jnp.where(mask, scores, 0.0)
    attn = jnp.einsum("hts,shd->thd", masked, value_full, precision=HIGH) + jnp.einsum(
        "thd,hde->the", query_full, state_before, precision=HIGH
    )
    inverse = lax.rsqrt(jnp.mean(attn * attn, axis=-1, keepdims=True) + 1e-05)
    normed = attn * inverse
    heads_out = normed.reshape(shard_len, head_count * head_width).astype(jnp.bfloat16)
    mixed_out = lax.psum_scatter(
        jnp.dot(heads_out, w_out, preferred_element_type=jnp.float32).astype(jnp.bfloat16),
        "tp",
        scatter_dimension=0,
        tiled=True,
    )
    grad_all = lax.all_gather(grad_out, "tp", axis=0, tiled=True)
    d_normed = lax.dot_general(grad_all, w_out, COLS_CONTRACT, preferred_element_type=jnp.float32)
    d_normed = d_normed.reshape(shard_len, head_count, head_width)
    d_attn = inverse * (d_normed - normed * jnp.mean(d_normed * normed, axis=-1, keepdims=True))
    local_adj = jnp.einsum("thd,the->hde", query_full, d_attn, precision=HIGH)
    _, later, adj_total = scanned(local_adj, "seq")
    rows_per = head_width // lax.axis_size("seq")
    state_grad = lax.dynamic_slice_in_dim(
        adj_total, lax.axis_index("seq") * rows_per, rows_per, axis=1
    )
    mixed_s = jnp.where(mask, jnp.einsum("the,she->hts", d_attn, value_full, precision=HIGH), 0.0)
    grad_q = jnp.einsum("the,hde->thd", d_attn, state_before, precision=HIGH) + jnp.einsum(
        "hts,shd->thd", mixed_s, key_full, precision=HIGH
    )
    grad_k = jnp.einsum("hts,thd->shd", mixed_s, query_full, precision=HIGH) + jnp.einsum(
        "hde,she->shd", later, value_full, precision=HIGH
    )
    grad_v = jnp.einsum("hts,the->she", masked, d_attn, precision=HIGH) + jnp.einsum(
        "hde,shd->she", later, key_full, precision=HIGH
    )
    query_grad = grad_q.reshape(shard_len, head_count * head_width).astype(jnp.bfloat16)
    key_grad = grad_k.reshape(shard_len, head_count * head_width).astype(jnp.bfloat16)
    value_grad = grad_v.reshape(shard_len, head_count * head_width).astype(jnp.bfloat16)
    term = lax.dot_general(query_grad, w_query, COLS_CONTRACT, preferred_element_type=jnp.float32)
    term = term + lax.dot_general(
        key_grad, w_key, COLS_CONTRACT, preferred_element_type=jnp.float32
    )
    input_grad = lax.psum_scatter(
        (
            term
            + lax.dot_general(
                value_grad, w_value, COLS_CONTRACT, preferred_element_type=jnp.float32
            )
        ).astype(jnp.bfloat16),
        "tp",
        scatter_dimension=0,
        tiled=True,
    )
    out_sum = grid_reduce_scatter(
        lax.dot_general(heads_out, grad_all, ROWS_CONTRACT, preferred_element_type=jnp.bfloat16),
        "seq",
        False,
        -1,
    )
    routes = ((True, 1), (True, -1), (False, 1), (False, -1))
    quarter = query_grad.shape[1] // len(routes)
    sums = []
    for index, (inner_first, shift) in enumerate(routes):
        cols = slice(index * quarter, (index + 1) * quarter)
        grads = jnp.concatenate([query_grad[:, cols], key_grad[:, cols], value_grad[:, cols]], axis=1)
        sums.append(
            grid_reduce_scatter(
                lax.dot_general(grads, rows_all, ROWS_CONTRACT, preferred_element_type=jnp.bfloat16),
                "seq",
                inner_first,
                shift,
            )
        )
    query_sum, key_sum, value_sum = (
        jnp.concatenate([part[k * quarter : (k + 1) * quarter] for part in sums], axis=0).T
        for k in range(3)
    )
    out_summed = out_sum
    grad_scale = lax.rsqrt(jnp.float32(shard_len * lax.axis_size("seq")))
    return (
        mixed_out,
        input_grad,
        query_sum.astype(jnp.float32) * grad_scale,
        key_sum.astype(jnp.float32) * grad_scale,
        value_sum.astype(jnp.float32) * grad_scale,
        out_summed.astype(jnp.float32) * grad_scale,
        state_grad,
    )


def solution(mesh):
    return jax.shard_map(
        body,
        mesh=mesh,
        in_specs=(
            P(("seq", "tp"), None),
            P(None, "tp"),
            P(None, "tp"),
            P(None, "tp"),
            P("tp", None),
            P("tp", None, None),
            P(("seq", "tp"), None),
        ),
        out_specs=(
            P(("seq", "tp"), None),
            P(("seq", "tp"), None),
            P("seq", "tp"),
            P("seq", "tp"),
            P("seq", "tp"),
            P("tp", "seq"),
            P("tp", "seq", None),
        ),
        check_vma=False,
    )
```

```python
import jax
import jax.numpy as jnp
from jax import lax
from jax.sharding import PartitionSpec as P

HIGH = lax.Precision.HIGHEST
ROWS_CONTRACT = (((0,), (0,)), ((), ()))
COLS_CONTRACT = (((1,), (1,)), ((), ()))


def scanned(array, axis):
    count = lax.axis_size(axis)
    place = lax.axis_index(axis)
    total = array
    before = jnp.zeros_like(array)
    after = jnp.zeros_like(array)
    step = 1
    while step < count:
        pairs = [(i, i ^ step) for i in range(count)]
        other = lax.ppermute(total, axis, pairs)
        upper = (place & step) != 0
        before = before + jnp.where(upper, other, 0.0)
        after = after + jnp.where(upper, 0.0, other)
        total = total + other
        step *= 2
    return before, after, total


RING = 4


def ring_pairs(count, shift, inner):
    pairs = []
    for place in range(count):
        outer, within = divmod(place, RING)
        if inner:
            target = outer * RING + (within + shift) % RING
        else:
            target = ((outer + shift) % (count // RING)) * RING + within
        pairs.append((place, target))
    return pairs


def ring_reduce_scatter(pieces, axis, inner, shift, strided):
    count = lax.axis_size(axis)
    place = lax.axis_index(axis)
    outer = count // RING
    ring = RING if inner else outer
    pos = place % RING if inner else place // RING
    pairs = ring_pairs(count, shift, inner)
    size = pieces.shape[1] // ring

    def piece(index):
        index = index % ring
        if strided:
            block = size // outer
            chunks = [
                lax.dynamic_slice_in_dim(pieces, group * size + index * block, block, 1)
                for group in range(outer)
            ]
            return jnp.concatenate(chunks, axis=1).astype(jnp.float32)
        return lax.dynamic_slice_in_dim(pieces, index * size, size, 1).astype(jnp.float32)

    acc = piece(pos - shift)
    for step in range(ring - 1):
        got = lax.ppermute(acc.astype(jnp.bfloat16), axis, pairs)
        acc = got.astype(jnp.float32) + piece(pos - (2 + step) * shift)
    return acc


def grid_reduce_scatter(partial, axis, inner_first, shift):
    partial = ring_reduce_scatter(partial, axis, inner_first, shift, inner_first)
    return ring_reduce_scatter(partial.astype(jnp.bfloat16), axis, not inner_first, shift, False)


def body(tokens, w_query, w_key, w_value, w_out, state_in, grad_out):
    head_count = state_in.shape[0]
    head_width = state_in.shape[1]
    rows_all = lax.all_gather(tokens, "tp", axis=0, tiled=True)
    shard_len = rows_all.shape[0]

    def head_split(matrix):
        return matrix.reshape(shard_len, head_count, head_width)

    query = jnp.dot(rows_all, w_query, preferred_element_type=jnp.float32).astype(jnp.bfloat16)
    key_all = jnp.dot(rows_all, w_key, preferred_element_type=jnp.float32).astype(jnp.bfloat16)
    value_all = jnp.dot(rows_all, w_value, preferred_element_type=jnp.float32).astype(jnp.bfloat16)
    query_heads = head_split(query)
    key_heads = head_split(key_all)
    value_heads = head_split(value_all)
    query_full = query_heads.astype(jnp.float32)
    key_full = key_heads.astype(jnp.float32)
    value_full = value_heads.astype(jnp.float32)
    local_kv = jnp.einsum(
        "thd,the->hde", key_heads, value_heads, preferred_element_type=jnp.float32
    )
    earlier, _, _ = scanned(local_kv, "seq")
    state_before = state_in + earlier
    row_ids = lax.broadcasted_iota(jnp.int32, (shard_len, shard_len), 0)
    col_ids = lax.broadcasted_iota(jnp.int32, (shard_len, shard_len), 1)
    mask = (row_ids >= col_ids)[None]
    scores = jnp.einsum("thd,shd->hts", query_heads, key_heads, preferred_element_type=jnp.float32)
    masked = jnp.where(mask, scores, 0.0)
    attn = jnp.einsum("hts,shd->thd", masked, value_full, precision=HIGH) + jnp.einsum(
        "thd,hde->the", query_full, state_before, precision=HIGH
    )
    inverse = lax.rsqrt(jnp.mean(attn * attn, axis=-1, keepdims=True) + 1e-05)
    normed = attn * inverse
    heads_out = normed.reshape(shard_len, head_count * head_width).astype(jnp.bfloat16)
    mixed_out = lax.psum_scatter(
        jnp.dot(heads_out, w_out, preferred_element_type=jnp.float32).astype(jnp.bfloat16),
        "tp",
        scatter_dimension=0,
        tiled=True,
    )
    grad_all = lax.all_gather(grad_out, "tp", axis=0, tiled=True)
    d_normed = lax.dot_general(grad_all, w_out, COLS_CONTRACT, preferred_element_type=jnp.float32)
    d_normed = d_normed.reshape(shard_len, head_count, head_width)
    d_attn = inverse * (d_normed - normed * jnp.mean(d_normed * normed, axis=-1, keepdims=True))
    local_adj = jnp.einsum("thd,the->hde", query_full, d_attn, precision=HIGH)
    _, later, adj_total = scanned(local_adj, "seq")
    rows_per = head_width // lax.axis_size("seq")
    state_grad = lax.dynamic_slice_in_dim(
        adj_total, lax.axis_index("seq") * rows_per, rows_per, axis=1
    )
    mixed_s = jnp.where(mask, jnp.einsum("the,she->hts", d_attn, value_full, precision=HIGH), 0.0)
    grad_q = jnp.einsum("the,hde->thd", d_attn, state_before, precision=HIGH) + jnp.einsum(
        "hts,shd->thd", mixed_s, key_full, precision=HIGH
    )
    grad_k = jnp.einsum("hts,thd->shd", mixed_s, query_full, precision=HIGH) + jnp.einsum(
        "hde,she->shd", later, value_full, precision=HIGH
    )
    grad_v = jnp.einsum("hts,the->she", masked, d_attn, precision=HIGH) + jnp.einsum(
        "hde,shd->she", later, key_full, precision=HIGH
    )
    query_grad = grad_q.reshape(shard_len, head_count * head_width).astype(jnp.bfloat16)
    key_grad = grad_k.reshape(shard_len, head_count * head_width).astype(jnp.bfloat16)
    value_grad = grad_v.reshape(shard_len, head_count * head_width).astype(jnp.bfloat16)
    term = lax.dot_general(query_grad, w_query, COLS_CONTRACT, preferred_element_type=jnp.float32)
    term = term + lax.dot_general(
        key_grad, w_key, COLS_CONTRACT, preferred_element_type=jnp.float32
    )
    input_grad = lax.psum_scatter(
        (
            term
            + lax.dot_general(
                value_grad, w_value, COLS_CONTRACT, preferred_element_type=jnp.float32
            )
        ).astype(jnp.bfloat16),
        "tp",
        scatter_dimension=0,
        tiled=True,
    )
    out_part = lax.dot_general(heads_out, grad_all, ROWS_CONTRACT, preferred_element_type=jnp.bfloat16)
    out_rows = out_part.shape[0] // 2
    out_sum = jnp.concatenate(
        [
            lax.psum_scatter(
                out_part[:out_rows], "seq", scatter_dimension=1, tiled=True
            ).astype(jnp.float32),
            grid_reduce_scatter(out_part[out_rows:], "seq", False, -1),
        ],
        axis=0,
    )
    routes = ((True, 1), (True, -1), (False, 1), (False, -1))
    quarter = query_grad.shape[1] // len(routes)
    sums = []
    for index, (inner_first, shift) in enumerate(routes):
        cols = slice(index * quarter, (index + 1) * quarter)
        grads = jnp.concatenate([query_grad[:, cols], key_grad[:, cols], value_grad[:, cols]], axis=1)
        sums.append(
            grid_reduce_scatter(
                lax.dot_general(grads, rows_all, ROWS_CONTRACT, preferred_element_type=jnp.bfloat16),
                "seq",
                inner_first,
                shift,
            )
        )
    query_sum, key_sum, value_sum = (
        jnp.concatenate([part[k * quarter : (k + 1) * quarter] for part in sums], axis=0).T
        for k in range(3)
    )
    out_summed = out_sum
    grad_scale = lax.rsqrt(jnp.float32(shard_len * lax.axis_size("seq")))
    return (
        mixed_out,
        input_grad,
        query_sum.astype(jnp.float32) * grad_scale,
        key_sum.astype(jnp.float32) * grad_scale,
        value_sum.astype(jnp.float32) * grad_scale,
        out_summed.astype(jnp.float32) * grad_scale,
        state_grad,
    )


def solution(mesh):
    return jax.shard_map(
        body,
        mesh=mesh,
        in_specs=(
            P(("seq", "tp"), None),
            P(None, "tp"),
            P(None, "tp"),
            P(None, "tp"),
            P("tp", None),
            P("tp", None, None),
            P(("seq", "tp"), None),
        ),
        out_specs=(
            P(("seq", "tp"), None),
            P(("seq", "tp"), None),
            P("seq", "tp"),
            P("seq", "tp"),
            P("seq", "tp"),
            P("tp", "seq"),
            P("tp", "seq", None),
        ),
        check_vma=False,
    )
```

```python
import jax
import jax.numpy as jnp
from jax import lax
from jax.sharding import Mesh, PartitionSpec as P

HIGH = lax.Precision.HIGHEST
ROWS_CONTRACT = (((0,), (0,)), ((), ()))
COLS_CONTRACT = (((1,), (1,)), ((), ()))


def scanned(array, axis):
    count = lax.axis_size(axis)
    place = lax.axis_index(axis)
    total = array
    before = jnp.zeros_like(array)
    after = jnp.zeros_like(array)
    step = 1
    while step < count:
        pairs = [(i, i ^ step) for i in range(count)]
        other = lax.ppermute(total, axis, pairs)
        upper = (place & step) != 0
        before = before + jnp.where(upper, other, 0.0)
        after = after + jnp.where(upper, 0.0, other)
        total = total + other
        step *= 2
    return before, after, total


RING = 4


def ring_pairs(count, shift, inner):
    pairs = []
    for place in range(count):
        outer, within = divmod(place, RING)
        if inner:
            target = outer * RING + (within + shift) % RING
        else:
            target = ((outer + shift) % (count // RING)) * RING + within
        pairs.append((place, target))
    return pairs


def ring_reduce_scatter(pieces, axis, inner, shift, strided):
    count = lax.axis_size(axis)
    place = lax.axis_index(axis)
    outer = count // RING
    ring = RING if inner else outer
    pos = place % RING if inner else place // RING
    pairs = ring_pairs(count, shift, inner)
    size = pieces.shape[1] // ring

    def piece(index):
        index = index % ring
        if strided:
            block = size // outer
            chunks = [
                lax.dynamic_slice_in_dim(pieces, group * size + index * block, block, 1)
                for group in range(outer)
            ]
            return jnp.concatenate(chunks, axis=1).astype(jnp.float32)
        return lax.dynamic_slice_in_dim(pieces, index * size, size, 1).astype(jnp.float32)

    acc = piece(pos - shift)
    for step in range(ring - 1):
        got = lax.ppermute(acc.astype(jnp.bfloat16), axis, pairs)
        acc = got.astype(jnp.float32) + piece(pos - (2 + step) * shift)
    return acc


def grid_reduce_scatter(partial, axis, inner_first, shift):
    partial = ring_reduce_scatter(partial, axis, inner_first, shift, inner_first)
    return ring_reduce_scatter(partial.astype(jnp.bfloat16), axis, not inner_first, shift, False)


def body(tokens, w_query, w_key, w_value, w_out, state_in, grad_out):
    head_count = state_in.shape[0]
    head_width = state_in.shape[1]
    rows_all = lax.all_gather(
        lax.all_gather(tokens, "core", axis=0, tiled=True), "x", axis=0, tiled=True
    )
    shard_len = rows_all.shape[0]

    def head_split(matrix):
        return matrix.reshape(shard_len, head_count, head_width)

    query = jnp.dot(rows_all, w_query, preferred_element_type=jnp.float32).astype(jnp.bfloat16)
    key_all = jnp.dot(rows_all, w_key, preferred_element_type=jnp.float32).astype(jnp.bfloat16)
    value_all = jnp.dot(rows_all, w_value, preferred_element_type=jnp.float32).astype(jnp.bfloat16)
    query_heads = head_split(query)
    key_heads = head_split(key_all)
    value_heads = head_split(value_all)
    query_full = query_heads.astype(jnp.float32)
    key_full = key_heads.astype(jnp.float32)
    value_full = value_heads.astype(jnp.float32)
    local_kv = jnp.einsum(
        "thd,the->hde", key_heads, value_heads, preferred_element_type=jnp.float32
    )
    earlier, _, _ = scanned(local_kv, "seq")
    state_before = state_in + earlier
    row_ids = lax.broadcasted_iota(jnp.int32, (shard_len, shard_len), 0)
    col_ids = lax.broadcasted_iota(jnp.int32, (shard_len, shard_len), 1)
    mask = (row_ids >= col_ids)[None]
    scores = jnp.einsum("thd,shd->hts", query_heads, key_heads, preferred_element_type=jnp.float32)
    masked = jnp.where(mask, scores, 0.0)
    attn = jnp.einsum("hts,shd->thd", masked, value_full, precision=HIGH) + jnp.einsum(
        "thd,hde->the", query_full, state_before, precision=HIGH
    )
    inverse = lax.rsqrt(jnp.mean(attn * attn, axis=-1, keepdims=True) + 1e-05)
    normed = attn * inverse
    heads_out = normed.reshape(shard_len, head_count * head_width).astype(jnp.bfloat16)
    mixed_out = lax.psum_scatter(
        jnp.dot(heads_out, w_out, preferred_element_type=jnp.float32).astype(jnp.bfloat16),
        ("x", "core"),
        scatter_dimension=0,
        tiled=True,
    )
    grad_all = lax.all_gather(
        lax.all_gather(grad_out, "core", axis=0, tiled=True), "x", axis=0, tiled=True
    )
    d_normed = lax.dot_general(grad_all, w_out, COLS_CONTRACT, preferred_element_type=jnp.float32)
    d_normed = d_normed.reshape(shard_len, head_count, head_width)
    d_attn = inverse * (d_normed - normed * jnp.mean(d_normed * normed, axis=-1, keepdims=True))
    local_adj = jnp.einsum("thd,the->hde", query_full, d_attn, precision=HIGH)
    _, later, adj_total = scanned(local_adj, "seq")
    rows_per = head_width // lax.axis_size("seq")
    state_grad = lax.dynamic_slice_in_dim(
        adj_total, lax.axis_index("seq") * rows_per, rows_per, axis=1
    )
    mixed_s = jnp.where(mask, jnp.einsum("the,she->hts", d_attn, value_full, precision=HIGH), 0.0)
    grad_q = jnp.einsum("the,hde->thd", d_attn, state_before, precision=HIGH) + jnp.einsum(
        "hts,shd->thd", mixed_s, key_full, precision=HIGH
    )
    grad_k = jnp.einsum("hts,thd->shd", mixed_s, query_full, precision=HIGH) + jnp.einsum(
        "hde,she->shd", later, value_full, precision=HIGH
    )
    grad_v = jnp.einsum("hts,the->she", masked, d_attn, precision=HIGH) + jnp.einsum(
        "hde,shd->she", later, key_full, precision=HIGH
    )
    query_grad = grad_q.reshape(shard_len, head_count * head_width).astype(jnp.bfloat16)
    key_grad = grad_k.reshape(shard_len, head_count * head_width).astype(jnp.bfloat16)
    value_grad = grad_v.reshape(shard_len, head_count * head_width).astype(jnp.bfloat16)
    term = lax.dot_general(query_grad, w_query, COLS_CONTRACT, preferred_element_type=jnp.float32)
    term = term + lax.dot_general(
        key_grad, w_key, COLS_CONTRACT, preferred_element_type=jnp.float32
    )
    input_grad = lax.psum_scatter(
        (
            term
            + lax.dot_general(
                value_grad, w_value, COLS_CONTRACT, preferred_element_type=jnp.float32
            )
        ).astype(jnp.bfloat16),
        ("x", "core"),
        scatter_dimension=0,
        tiled=True,
    )
    out_sum = grid_reduce_scatter(
        lax.dot_general(heads_out, grad_all, ROWS_CONTRACT, preferred_element_type=jnp.bfloat16),
        "seq",
        False,
        -1,
    )
    routes = ((True, 1), (True, -1), (False, 1), (False, -1))
    quarter = query_grad.shape[1] // len(routes)
    sums = []
    for index, (inner_first, shift) in enumerate(routes):
        cols = slice(index * quarter, (index + 1) * quarter)
        grads = jnp.concatenate([query_grad[:, cols], key_grad[:, cols], value_grad[:, cols]], axis=1)
        sums.append(
            grid_reduce_scatter(
                lax.dot_general(grads, rows_all, ROWS_CONTRACT, preferred_element_type=jnp.bfloat16),
                "seq",
                inner_first,
                shift,
            )
        )
    query_sum, key_sum, value_sum = (
        jnp.concatenate([part[k * quarter : (k + 1) * quarter] for part in sums], axis=0).T
        for k in range(3)
    )
    out_summed = out_sum
    grad_scale = lax.rsqrt(jnp.float32(shard_len * lax.axis_size("seq")))
    return (
        mixed_out,
        input_grad,
        query_sum.astype(jnp.float32) * grad_scale,
        key_sum.astype(jnp.float32) * grad_scale,
        value_sum.astype(jnp.float32) * grad_scale,
        out_summed.astype(jnp.float32) * grad_scale,
        state_grad,
    )


def solution(mesh):
    cores = 2
    split = Mesh(
        mesh.devices.reshape(mesh.shape["seq"], mesh.shape["tp"] // cores, cores),
        ("seq", "x", "core"),
    )
    return jax.shard_map(
        body,
        mesh=split,
        in_specs=(
            P(("seq", "x", "core"), None),
            P(None, ("x", "core")),
            P(None, ("x", "core")),
            P(None, ("x", "core")),
            P(("x", "core"), None),
            P(("x", "core"), None, None),
            P(("seq", "x", "core"), None),
        ),
        out_specs=(
            P(("seq", "x", "core"), None),
            P(("seq", "x", "core"), None),
            P("seq", ("x", "core")),
            P("seq", ("x", "core")),
            P("seq", ("x", "core")),
            P(("x", "core"), "seq"),
            P(("x", "core"), "seq", None),
        ),
        check_vma=False,
    )
```

```python
import jax
import jax.numpy as jnp
from jax import lax
from jax.sharding import PartitionSpec as P

HIGH = lax.Precision.HIGHEST
ROWS_CONTRACT = (((0,), (0,)), ((), ()))
COLS_CONTRACT = (((1,), (1,)), ((), ()))


def scanned(array, axis):
    count = lax.axis_size(axis)
    place = lax.axis_index(axis)
    total = array
    before = jnp.zeros_like(array)
    after = jnp.zeros_like(array)
    step = 1
    while step < count:
        pairs = [(i, i ^ step) for i in range(count)]
        other = lax.ppermute(total, axis, pairs)
        upper = (place & step) != 0
        before = before + jnp.where(upper, other, 0.0)
        after = after + jnp.where(upper, 0.0, other)
        total = total + other
        step *= 2
    return before, after, total


RING = 4


def ring_pairs(count, shift, inner):
    pairs = []
    for place in range(count):
        outer, within = divmod(place, RING)
        if inner:
            target = outer * RING + (within + shift) % RING
        else:
            target = ((outer + shift) % (count // RING)) * RING + within
        pairs.append((place, target))
    return pairs


def ring_reduce_scatter(pieces, axis, inner, shift, strided):
    count = lax.axis_size(axis)
    place = lax.axis_index(axis)
    outer = count // RING
    ring = RING if inner else outer
    pos = place % RING if inner else place // RING
    pairs = ring_pairs(count, shift, inner)
    size = pieces.shape[1] // ring

    def piece(index):
        index = index % ring
        if strided:
            block = size // outer
            chunks = [
                lax.dynamic_slice_in_dim(pieces, group * size + index * block, block, 1)
                for group in range(outer)
            ]
            return jnp.concatenate(chunks, axis=1).astype(jnp.float32)
        return lax.dynamic_slice_in_dim(pieces, index * size, size, 1).astype(jnp.float32)

    acc = piece(pos - shift)
    for step in range(ring - 1):
        got = lax.ppermute(acc.astype(jnp.bfloat16), axis, pairs)
        acc = got.astype(jnp.float32) + piece(pos - (2 + step) * shift)
    return acc


def joint_rings(sources, axis, routes, strided):
    count = lax.axis_size(axis)
    place = lax.axis_index(axis)
    outer = count // RING

    def setup(source, inner, shift, flag):
        ring = RING if inner else outer
        pos = place % RING if inner else place // RING
        size = source.shape[1] // ring

        def piece(index):
            index = index % ring
            if flag:
                block = size // outer
                chunks = [
                    lax.dynamic_slice_in_dim(source, group * size + index * block, block, 1)
                    for group in range(outer)
                ]
                return jnp.concatenate(chunks, axis=1).astype(jnp.float32)
            return lax.dynamic_slice_in_dim(source, index * size, size, 1).astype(jnp.float32)

        return pos, piece, ring_pairs(count, shift, inner)

    rings = [setup(src, inner, shift, flag) for src, (inner, shift), flag in zip(sources, routes, strided)]
    accs = tuple(piece(pos - shift) for (pos, piece, _), (_, shift) in zip(rings, routes))

    def step(index, accs):
        return tuple(
            lax.ppermute(acc.astype(jnp.bfloat16), axis, pairs).astype(jnp.float32)
            + piece(pos - (2 + index) * shift)
            for acc, (pos, piece, pairs), (_, shift) in zip(accs, rings, routes)
        )

    return lax.fori_loop(0, RING - 1, step, accs)


def grid_reduce_scatter(partial, axis, inner_first, shift):
    partial = ring_reduce_scatter(partial, axis, inner_first, shift, inner_first)
    return ring_reduce_scatter(partial.astype(jnp.bfloat16), axis, not inner_first, shift, False)


def body(tokens, w_query, w_key, w_value, w_out, state_in, grad_out):
    head_count = state_in.shape[0]
    head_width = state_in.shape[1]
    rows_all = lax.all_gather(tokens, "tp", axis=0, tiled=True)
    shard_len = rows_all.shape[0]

    def head_split(matrix):
        return matrix.reshape(shard_len, head_count, head_width)

    query = jnp.dot(rows_all, w_query, preferred_element_type=jnp.float32).astype(jnp.bfloat16)
    key_all = jnp.dot(rows_all, w_key, preferred_element_type=jnp.float32).astype(jnp.bfloat16)
    value_all = jnp.dot(rows_all, w_value, preferred_element_type=jnp.float32).astype(jnp.bfloat16)
    query_heads = head_split(query)
    key_heads = head_split(key_all)
    value_heads = head_split(value_all)
    query_full = query_heads.astype(jnp.float32)
    key_full = key_heads.astype(jnp.float32)
    value_full = value_heads.astype(jnp.float32)
    local_kv = jnp.einsum(
        "thd,the->hde", key_heads, value_heads, preferred_element_type=jnp.float32
    )
    earlier, _, _ = scanned(local_kv, "seq")
    state_before = state_in + earlier
    row_ids = lax.broadcasted_iota(jnp.int32, (shard_len, shard_len), 0)
    col_ids = lax.broadcasted_iota(jnp.int32, (shard_len, shard_len), 1)
    mask = (row_ids >= col_ids)[None]
    scores = jnp.einsum("thd,shd->hts", query_heads, key_heads, preferred_element_type=jnp.float32)
    masked = jnp.where(mask, scores, 0.0)
    attn = jnp.einsum("hts,shd->thd", masked, value_full, precision=HIGH) + jnp.einsum(
        "thd,hde->the", query_full, state_before, precision=HIGH
    )
    inverse = lax.rsqrt(jnp.mean(attn * attn, axis=-1, keepdims=True) + 1e-05)
    normed = attn * inverse
    heads_out = normed.reshape(shard_len, head_count * head_width).astype(jnp.bfloat16)
    mixed_out = lax.psum_scatter(
        jnp.dot(heads_out, w_out, preferred_element_type=jnp.float32).astype(jnp.bfloat16),
        "tp",
        scatter_dimension=0,
        tiled=True,
    )
    grad_all = lax.all_gather(grad_out, "tp", axis=0, tiled=True)
    d_normed = lax.dot_general(grad_all, w_out, COLS_CONTRACT, preferred_element_type=jnp.float32)
    d_normed = d_normed.reshape(shard_len, head_count, head_width)
    d_attn = inverse * (d_normed - normed * jnp.mean(d_normed * normed, axis=-1, keepdims=True))
    local_adj = jnp.einsum("thd,the->hde", query_full, d_attn, precision=HIGH)
    _, later, adj_total = scanned(local_adj, "seq")
    rows_per = head_width // lax.axis_size("seq")
    state_grad = lax.dynamic_slice_in_dim(
        adj_total, lax.axis_index("seq") * rows_per, rows_per, axis=1
    )
    mixed_s = jnp.where(mask, jnp.einsum("the,she->hts", d_attn, value_full, precision=HIGH), 0.0)
    grad_q = jnp.einsum("the,hde->thd", d_attn, state_before, precision=HIGH) + jnp.einsum(
        "hts,shd->thd", mixed_s, key_full, precision=HIGH
    )
    grad_k = jnp.einsum("hts,thd->shd", mixed_s, query_full, precision=HIGH) + jnp.einsum(
        "hde,she->shd", later, value_full, precision=HIGH
    )
    grad_v = jnp.einsum("hts,the->she", masked, d_attn, precision=HIGH) + jnp.einsum(
        "hde,shd->she", later, key_full, precision=HIGH
    )
    query_grad = grad_q.reshape(shard_len, head_count * head_width).astype(jnp.bfloat16)
    key_grad = grad_k.reshape(shard_len, head_count * head_width).astype(jnp.bfloat16)
    value_grad = grad_v.reshape(shard_len, head_count * head_width).astype(jnp.bfloat16)
    term = lax.dot_general(query_grad, w_query, COLS_CONTRACT, preferred_element_type=jnp.float32)
    term = term + lax.dot_general(
        key_grad, w_key, COLS_CONTRACT, preferred_element_type=jnp.float32
    )
    input_grad = lax.psum_scatter(
        (
            term
            + lax.dot_general(
                value_grad, w_value, COLS_CONTRACT, preferred_element_type=jnp.float32
            )
        ).astype(jnp.bfloat16),
        "tp",
        scatter_dimension=0,
        tiled=True,
    )
    out_sum = grid_reduce_scatter(
        lax.dot_general(heads_out, grad_all, ROWS_CONTRACT, preferred_element_type=jnp.bfloat16),
        "seq",
        False,
        -1,
    )
    routes = ((True, 1), (True, -1), (False, 1), (False, -1))
    quarter = query_grad.shape[1] // len(routes)
    partials = []
    for index in range(len(routes)):
        cols = slice(index * quarter, (index + 1) * quarter)
        grads = jnp.concatenate([query_grad[:, cols], key_grad[:, cols], value_grad[:, cols]], axis=1)
        partials.append(
            lax.dot_general(grads, rows_all, ROWS_CONTRACT, preferred_element_type=jnp.bfloat16)
        )
    firsts = joint_rings(partials, "seq", routes, [inner for inner, _ in routes])
    sums = joint_rings(
        [part.astype(jnp.bfloat16) for part in firsts],
        "seq",
        [(not inner, shift) for inner, shift in routes],
        [False] * len(routes),
    )
    query_sum, key_sum, value_sum = (
        jnp.concatenate([part[k * quarter : (k + 1) * quarter] for part in sums], axis=0).T
        for k in range(3)
    )
    out_summed = out_sum
    grad_scale = lax.rsqrt(jnp.float32(shard_len * lax.axis_size("seq")))
    return (
        mixed_out,
        input_grad,
        query_sum.astype(jnp.float32) * grad_scale,
        key_sum.astype(jnp.float32) * grad_scale,
        value_sum.astype(jnp.float32) * grad_scale,
        out_summed.astype(jnp.float32) * grad_scale,
        state_grad,
    )


def solution(mesh):
    return jax.shard_map(
        body,
        mesh=mesh,
        in_specs=(
            P(("seq", "tp"), None),
            P(None, "tp"),
            P(None, "tp"),
            P(None, "tp"),
            P("tp", None),
            P("tp", None, None),
            P(("seq", "tp"), None),
        ),
        out_specs=(
            P(("seq", "tp"), None),
            P(("seq", "tp"), None),
            P("seq", "tp"),
            P("seq", "tp"),
            P("seq", "tp"),
            P("tp", "seq"),
            P("tp", "seq", None),
        ),
        check_vma=False,
    )
```

```python
import jax
import jax.numpy as jnp
from jax import lax
from jax.sharding import PartitionSpec as P

HIGH = lax.Precision.HIGHEST
ROWS_CONTRACT = (((0,), (0,)), ((), ()))
COLS_CONTRACT = (((1,), (1,)), ((), ()))


def scanned(array, axis):
    count = lax.axis_size(axis)
    place = lax.axis_index(axis)
    total = array
    before = jnp.zeros_like(array)
    after = jnp.zeros_like(array)
    step = 1
    while step < count:
        pairs = [(i, i ^ step) for i in range(count)]
        other = lax.ppermute(total, axis, pairs)
        upper = (place & step) != 0
        before = before + jnp.where(upper, other, 0.0)
        after = after + jnp.where(upper, 0.0, other)
        total = total + other
        step *= 2
    return before, after, total


RING = 4


def ring_pairs(count, shift, inner):
    pairs = []
    for place in range(count):
        outer, within = divmod(place, RING)
        if inner:
            target = outer * RING + (within + shift) % RING
        else:
            target = ((outer + shift) % (count // RING)) * RING + within
        pairs.append((place, target))
    return pairs


def ring_reduce_scatter(pieces, axis, inner, shift, strided):
    count = lax.axis_size(axis)
    place = lax.axis_index(axis)
    outer = count // RING
    ring = RING if inner else outer
    pos = place % RING if inner else place // RING
    pairs = ring_pairs(count, shift, inner)
    size = pieces.shape[1] // ring

    def piece(index):
        index = index % ring
        if strided:
            block = size // outer
            chunks = [
                lax.dynamic_slice_in_dim(pieces, group * size + index * block, block, 1)
                for group in range(outer)
            ]
            return jnp.concatenate(chunks, axis=1).astype(jnp.float32)
        return lax.dynamic_slice_in_dim(pieces, index * size, size, 1).astype(jnp.float32)

    acc = piece(pos - shift)
    for step in range(ring - 1):
        got = lax.ppermute(acc.astype(jnp.bfloat16), axis, pairs)
        acc = got.astype(jnp.float32) + piece(pos - (2 + step) * shift)
    return acc


def grid_reduce_scatter(partial, axis, inner_first, shift):
    partial = ring_reduce_scatter(partial, axis, inner_first, shift, inner_first)
    return ring_reduce_scatter(partial.astype(jnp.bfloat16), axis, not inner_first, shift, False)


def body(tokens, w_query, w_key, w_value, w_out, state_in, grad_out):
    head_count = state_in.shape[0]
    head_width = state_in.shape[1]
    rows_all = lax.all_gather(tokens, "tp", axis=0, tiled=True)
    shard_len = rows_all.shape[0]

    def head_split(matrix):
        return matrix.reshape(shard_len, head_count, head_width)

    query = jnp.dot(rows_all, w_query, preferred_element_type=jnp.float32).astype(jnp.bfloat16)
    key_all = jnp.dot(rows_all, w_key, preferred_element_type=jnp.float32).astype(jnp.bfloat16)
    value_all = jnp.dot(rows_all, w_value, preferred_element_type=jnp.float32).astype(jnp.bfloat16)
    query_heads = head_split(query)
    key_heads = head_split(key_all)
    value_heads = head_split(value_all)
    query_full = query_heads.astype(jnp.float32)
    key_full = key_heads.astype(jnp.float32)
    value_full = value_heads.astype(jnp.float32)
    local_kv = jnp.einsum(
        "thd,the->hde", key_heads, value_heads, preferred_element_type=jnp.float32
    )
    earlier, _, _ = scanned(local_kv, "seq")
    state_before = state_in + earlier
    row_ids = lax.broadcasted_iota(jnp.int32, (shard_len, shard_len), 0)
    col_ids = lax.broadcasted_iota(jnp.int32, (shard_len, shard_len), 1)
    mask = (row_ids >= col_ids)[None]
    scores = jnp.einsum("thd,shd->hts", query_heads, key_heads, preferred_element_type=jnp.float32)
    masked = jnp.where(mask, scores, 0.0)
    attn = jnp.einsum("hts,shd->thd", masked, value_full, precision=HIGH) + jnp.einsum(
        "thd,hde->the", query_full, state_before, precision=HIGH
    )
    inverse = lax.rsqrt(jnp.mean(attn * attn, axis=-1, keepdims=True) + 1e-05)
    normed = attn * inverse
    heads_out = normed.reshape(shard_len, head_count * head_width).astype(jnp.bfloat16)
    mixed_out = lax.psum_scatter(
        jnp.dot(heads_out, w_out, preferred_element_type=jnp.float32).astype(jnp.bfloat16),
        "tp",
        scatter_dimension=0,
        tiled=True,
    )
    grad_all = lax.all_gather(grad_out, "tp", axis=0, tiled=True)
    d_normed = lax.dot_general(grad_all, w_out, COLS_CONTRACT, preferred_element_type=jnp.float32)
    d_normed = d_normed.reshape(shard_len, head_count, head_width)
    d_attn = inverse * (d_normed - normed * jnp.mean(d_normed * normed, axis=-1, keepdims=True))
    local_adj = jnp.einsum("thd,the->hde", query_full, d_attn, precision=HIGH)
    _, later, adj_total = scanned(local_adj, "seq")
    rows_per = head_width // lax.axis_size("seq")
    state_grad = lax.dynamic_slice_in_dim(
        adj_total, lax.axis_index("seq") * rows_per, rows_per, axis=1
    )
    mixed_s = jnp.where(mask, jnp.einsum("the,she->hts", d_attn, value_full, precision=HIGH), 0.0)
    grad_q = jnp.einsum("the,hde->thd", d_attn, state_before, precision=HIGH) + jnp.einsum(
        "hts,shd->thd", mixed_s, key_full, precision=HIGH
    )
    grad_k = jnp.einsum("hts,thd->shd", mixed_s, query_full, precision=HIGH) + jnp.einsum(
        "hde,she->shd", later, value_full, precision=HIGH
    )
    grad_v = jnp.einsum("hts,the->she", masked, d_attn, precision=HIGH) + jnp.einsum(
        "hde,shd->she", later, key_full, precision=HIGH
    )
    query_grad = grad_q.reshape(shard_len, head_count * head_width).astype(jnp.bfloat16)
    key_grad = grad_k.reshape(shard_len, head_count * head_width).astype(jnp.bfloat16)
    value_grad = grad_v.reshape(shard_len, head_count * head_width).astype(jnp.bfloat16)
    term = lax.dot_general(query_grad, w_query, COLS_CONTRACT, preferred_element_type=jnp.float32)
    term = term + lax.dot_general(
        key_grad, w_key, COLS_CONTRACT, preferred_element_type=jnp.float32
    )
    input_grad = lax.psum_scatter(
        (
            term
            + lax.dot_general(
                value_grad, w_value, COLS_CONTRACT, preferred_element_type=jnp.float32
            )
        ).astype(jnp.bfloat16),
        "tp",
        scatter_dimension=0,
        tiled=True,
    )
    out_part = lax.dot_general(heads_out, grad_all, ROWS_CONTRACT, preferred_element_type=jnp.bfloat16)
    out_rows = out_part.shape[0] // 2
    out_sum = jnp.concatenate(
        [
            grid_reduce_scatter(out_part[:out_rows], "seq", False, -1),
            grid_reduce_scatter(out_part[out_rows:], "seq", True, 1),
        ],
        axis=0,
    )
    routes = ((True, 1), (True, -1), (False, 1), (False, -1))
    quarter = query_grad.shape[1] // len(routes)
    sums = []
    for index, (inner_first, shift) in enumerate(routes):
        cols = slice(index * quarter, (index + 1) * quarter)
        grads = jnp.concatenate([query_grad[:, cols], key_grad[:, cols], value_grad[:, cols]], axis=1)
        sums.append(
            grid_reduce_scatter(
                lax.dot_general(grads, rows_all, ROWS_CONTRACT, preferred_element_type=jnp.bfloat16),
                "seq",
                inner_first,
                shift,
            )
        )
    query_sum, key_sum, value_sum = (
        jnp.concatenate([part[k * quarter : (k + 1) * quarter] for part in sums], axis=0).T
        for k in range(3)
    )
    out_summed = out_sum
    grad_scale = lax.rsqrt(jnp.float32(shard_len * lax.axis_size("seq")))
    return (
        mixed_out,
        input_grad,
        query_sum.astype(jnp.float32) * grad_scale,
        key_sum.astype(jnp.float32) * grad_scale,
        value_sum.astype(jnp.float32) * grad_scale,
        out_summed.astype(jnp.float32) * grad_scale,
        state_grad,
    )


def solution(mesh):
    return jax.shard_map(
        body,
        mesh=mesh,
        in_specs=(
            P(("seq", "tp"), None),
            P(None, "tp"),
            P(None, "tp"),
            P(None, "tp"),
            P("tp", None),
            P("tp", None, None),
            P(("seq", "tp"), None),
        ),
        out_specs=(
            P(("seq", "tp"), None),
            P(("seq", "tp"), None),
            P("seq", "tp"),
            P("seq", "tp"),
            P("seq", "tp"),
            P("tp", "seq"),
            P("tp", "seq", None),
        ),
        check_vma=False,
    )
```
